128 devices in a mesh: seq: 16 (over x, y), exp: 8 (over z, core).
Axes of the slice: x: 4, y: 4, z: 4, core: 2. Of those that a mesh axis runs over, the one named last changes fastest.
Arguments:
- hidden: bfloat16 [2048, 4096], P('seq', 'exp'), may hold values from -6 to 6
- queries: bfloat16 [2048, 4096], P('seq', 'exp'), may hold values from -40 to 40
- keys: bfloat16 [2048, 1024], P('seq', 'exp'), may hold values from -6 to 6
- values: bfloat16 [2048, 1024], P('seq', 'exp'), may hold values from -6 to 6
- block_place: int32 [32], replicated, may hold values from 0 to 31, as said below
- page_table: int32 [128], replicated, may hold values from 0 to 127, each once
- out_weight: bfloat16 [4096, 4096], P('exp'), may hold values from -0.09375 to 0.09375
- norm_gain: float32 [4096], replicated, may hold values from 0.5 to 2
- gate_probs: float32 [2048, 2], P('seq'), may hold values from 0.1 to 1
- routes: int32 [2048, 2], P('seq'), may hold values from 0 to 7, all different within a row; in each aligned block of 128 rows (0 to 127, 128 to 255, ...) at most 64 rows name the same one
- w_gate: bfloat16 [8, 4096, 14336], P('exp', None, 'seq'), may hold values from -0.09375 to 0.09375
- w_up: bfloat16 [8, 4096, 14336], P('exp', None, 'seq'), may hold values from -0.09375 to 0.09375
- w_down: bfloat16 [8, 14336, 4096], P('exp', 'seq'), may hold values from -0.046875 to 0.046875
Outputs:
- layer_out: bfloat16 [2048, 4096], P('seq', 'exp')
- key_value_pages: bfloat16 [128, 16, 2, 1024], P('seq', None, None, 'exp')
The draws below stay inside these ranges and needn't reach their ends.
Inputs may be any that keep to these rules, and one draw needn't show every extreme that they name: `block_place`: the first 24 entries are a permutation of 0 to 23, the others a permutation of 24 to 31. `page_table`: A permutation of the pages. `routes`: in the rows of one index of seq (128 rows) no expert is named more than 64 times, a bound that some block reaches; a row names two different experts.
All inputs are finite; a program needn't handle non-finite values.
Results may differ from the reference program's by a relative error of at most 0.02.
Values may be sent and summed in bfloat16 or wider, within the bound.
No kernel may reach another device: no remote copies, remote signals or barrier semaphores. Data moves between devices by JAX's collectives and lax.ppermute only.
A program may use at most 128 MiB of HBM per device.

```python
import math
import jax
import jax.numpy as jnp
import numpy as np
from jax import lax

D = 4096
QUERY_HEADS = 32
KEY_VALUE_HEADS = 8
HEAD_SIZE = 128
NEXP = 8
TOP = 2
FF = 14336
TOKENS_PER_SEQ = 128
PAGE_TOKENS = 16
HALF = 64
CAP = 64
PROMPT_TOKENS = 2048
LONG = 1536
BLOCKS = 32
LONG_BLOCKS = 24
PAGE_TOTAL = 128


def key_region(key):
    random_subkey = jax.random.fold_in(key, 11)
    return jnp.clip(jax.random.normal(random_subkey, (PROMPT_TOKENS, KEY_VALUE_HEADS * HEAD_SIZE), jnp.float32), -6.0, 6.0)


def draw_keys(key, part):
    return key_region(key).astype(jnp.bfloat16)


def draw_queries(key, part):
    base_field = jnp.clip(jax.random.normal(jax.random.fold_in(key, 23), (PROMPT_TOKENS, QUERY_HEADS * HEAD_SIZE), jnp.float32), -6.0, 6.0)
    return base_field.astype(jnp.bfloat16)


def draw_block_place(key, part):
    long_order = jax.random.permutation(jax.random.fold_in(key, 31), LONG_BLOCKS).astype(jnp.int32)
    short_order = jax.random.permutation(jax.random.fold_in(key, 37), BLOCKS - LONG_BLOCKS).astype(jnp.int32) + LONG_BLOCKS
    return jnp.concatenate([long_order, short_order]).astype(jnp.int32)


def block_scale(rng, dims, split, smallest, largest):
    factor_of = 1.0
    for axis_at, parts in split:
        heights = jax.random.uniform(jax.random.fold_in(jax.random.fold_in(rng, 6), axis_at), (parts,), jnp.float32, smallest / len(split), largest / len(split))
        factor_of = factor_of * jnp.repeat(jnp.exp(heights), dims[axis_at] // parts).reshape((-1,) + (1,) * (len(dims) - 1 - axis_at))
    return factor_of


def assign_block(key, own, number, rows, number_of, top, bound, skew):
    ranking = jax.random.permutation(key, number_of)
    heavy_load, usual = shares(number_of, rows * top, bound, skew, True), shares(number_of, rows * top, bound, skew, False)
    places = jnp.arange(number_of)

    def named(tallies, turn):
        used = int((tallies > 0).sum())
        fixed = max(1, used // 4)
        shifted = fixed + (places - fixed + turn * (used - fixed)) % max(1, number_of - fixed)
        return jnp.zeros((number_of,), jnp.int32).at[ranking[jnp.where(places < fixed, places, shifted)]].set(jnp.asarray(tallies, jnp.int32))

    tallies = jnp.where(number % 4 == 0, named(heavy_load, number // 4), named(usual, number - number // 4 - 1))
    mixed = jax.random.permutation(jax.random.fold_in(own, 3), number_of)
    source_of, receiver = mixed[0:number_of // 2 * 2:2], mixed[1:number_of // 2 * 2:2]
    room = jnp.minimum(tallies[source_of] - 1, bound - tallies[receiver]) // 2
    room = jnp.where((source_of == ranking[0]) | (receiver == ranking[0]) | (tallies[receiver] == 0), 0, jnp.maximum(room, 0))
    shifted = jax.random.randint(jax.random.fold_in(own, 4), (number_of // 2,), 0, 1 << 20) % (room + 1)
    tallies = tallies.at[source_of].add(-shifted).at[receiver].add(shifted)
    items = jnp.searchsorted(jnp.cumsum(tallies), jnp.arange(rows * top), side="right").astype(jnp.int32)
    listing = items.reshape(top, rows).T
    listing = listing[jax.random.permutation(jax.random.fold_in(own, 1), rows)]
    turn = jax.random.randint(jax.random.fold_in(own, 2), (rows, 1), 0, top)
    return jnp.take_along_axis(listing, (jnp.arange(top)[None, :] + turn) % top, axis=1)


def shares(number_of, total, reach, slope, full):
    weights = [(1 << 20) // math.isqrt(grade ** slope) + 1 for grade in range(1, number_of + 1)]
    largest = reach if full else min(reach, max(-(-total // number_of), total * weights[0] // sum(weights)))
    least = 1 if total - largest >= number_of - 1 else 0
    holding, rest = [largest] + [least] * (number_of - 1), total - largest - least * (number_of - 1)
    while rest > 0:
        movable = [i for i in range(1, number_of) if holding[i] < largest] or [i for i in range(1, number_of) if holding[i] < reach]
        pool, budget = sum([weights[i] for i in movable]), rest
        for i in movable:
            more = min(reach - holding[i], max(1, budget * weights[i] // pool), rest)
            holding[i] = holding[i] + more
            rest = rest - more
    return np.array(holding)


def gaussian(key, dims, deviation, most, pieces=(), held_as=jnp.bfloat16):
    loudness = block_scale(key, dims, pieces, -0.22, 0.18) if pieces else 1.0
    values = jax.random.normal(key, dims, jnp.float32) * deviation * loudness
    return jnp.minimum(jnp.maximum(values, -most), most).astype(held_as)


def setup_inputs(seed: int = 0) -> dict:
    splits = jax.random.split(jax.random.key(seed), 14)
    hidden = gaussian(splits[0], (PROMPT_TOKENS, D), 1.0, 6.0, ((0, 16), (1, 8)))
    queries = draw_queries(jax.random.fold_in(splits[13], 71), 0)
    keys = draw_keys(jax.random.fold_in(splits[13], 71), 0)
    values = gaussian(splits[3], (PROMPT_TOKENS, KEY_VALUE_HEADS * HEAD_SIZE), 1.0, 6.0, ((0, 16), (1, 8)))
    block_place = draw_block_place(jax.random.fold_in(splits[13], 71), 0)
    page_table = jax.random.permutation(splits[5], PAGE_TOTAL).astype(jnp.int32)
    out_weight = gaussian(splits[6], (QUERY_HEADS * HEAD_SIZE, D), (QUERY_HEADS * HEAD_SIZE) ** -0.5, 0.09375, ((0, 8),))
    norm_gain = jnp.clip(jnp.exp(jax.random.uniform(splits[7], (D,), jnp.float32, math.log(0.5), math.log(2.0))), 0.5, 2.0)
    gate_probs = jnp.clip(jnp.exp(math.log(1.0) - 2.3025851 * jax.random.uniform(splits[8], (PROMPT_TOKENS, TOP), jnp.float32) ** block_scale(splits[8], (PROMPT_TOKENS, TOP), ((0, 16),), -0.2, 0.2)), 0.1, 1.0)
    routes_keys = jax.random.split(jax.random.fold_in(splits[9], 1), PROMPT_TOKENS // TOKENS_PER_SEQ)
    routes_turns = jax.random.permutation(jax.random.fold_in(splits[9], 3), PROMPT_TOKENS // TOKENS_PER_SEQ)
    routes = jax.vmap(lambda own, number: assign_block(jax.random.fold_in(splits[9], 2), own, number, TOKENS_PER_SEQ, NEXP, TOP, CAP, 2))(routes_keys, routes_turns).reshape((PROMPT_TOKENS, TOP))
    w_gate = gaussian(splits[10], (NEXP, D, FF), D ** -0.5, 0.09375, ((0, 8), (2, 16)))
    w_up = gaussian(splits[11], (NEXP, D, FF), D ** -0.5, 0.09375, ((0, 8), (2, 16)))
    w_down = gaussian(splits[12], (NEXP, FF, D), FF ** -0.5, 0.046875, ((0, 8), (1, 16)))
    return dict(hidden=hidden, queries=queries, keys=keys, values=values, block_place=block_place, page_table=page_table, out_weight=out_weight, norm_gain=norm_gain, gate_probs=gate_probs, routes=routes, w_gate=w_gate, w_up=w_up, w_down=w_down)


THETA = 1000000.0
EPS = 1e-05

def apply_rotary(values_in, positions, head_count):
    row_count = values_in.shape[0]
    split_view = values_in.astype(jnp.float32).reshape(row_count, head_count, HEAD_SIZE)
    steps_half = jnp.arange(HEAD_SIZE // 2, dtype=jnp.float32)
    frequency = THETA ** (-(2.0 * steps_half) / HEAD_SIZE)
    angles = positions.astype(jnp.float32)[:, None] * frequency[None, :]
    cosine = jnp.cos(angles)[:, None, :]
    sine_part = jnp.sin(angles)[:, None, :]
    front_half = split_view[..., :HEAD_SIZE // 2]
    back_half = split_view[..., HEAD_SIZE // 2:]
    turned = jnp.concatenate([front_half * cosine - back_half * sine_part, back_half * cosine + front_half * sine_part], axis=-1)
    return turned.reshape(row_count, head_count * HEAD_SIZE).astype(jnp.bfloat16)

def expert_outputs(normed, routes, w_gate, w_up, w_down):
    assign_count = PROMPT_TOKENS * TOP
    flat_routes = routes.reshape(assign_count).astype(jnp.int32)
    order = jnp.argsort(flat_routes, stable=True).astype(jnp.int32)
    sorted_expert = flat_routes[order]
    sorted_rows = normed[order // TOP]
    block_rows = min(128, assign_count)

    def one_block(block_index):
        row_block = lax.dynamic_slice_in_dim(sorted_rows, block_index * block_rows, block_rows)
        expert_block = lax.dynamic_slice_in_dim(sorted_expert, block_index * block_rows, block_rows)

        def per_expert(expert_id, running):
            gate_part = jnp.dot(row_block, w_gate[expert_id], preferred_element_type=jnp.float32)
            up_part = jnp.dot(row_block, w_up[expert_id], preferred_element_type=jnp.float32)
            units = (jax.nn.silu(gate_part) * up_part).astype(jnp.bfloat16)
            result = jnp.dot(units, w_down[expert_id], preferred_element_type=jnp.float32)
            return jnp.where((expert_block == expert_id)[:, None], result, running)
        return lax.fori_loop(expert_block[0], expert_block[block_rows - 1] + 1, per_expert, jnp.zeros((block_rows, D), jnp.float32))
    outputs = lax.map(one_block, jnp.arange(assign_count // block_rows, dtype=jnp.int32))
    outputs = outputs.reshape(assign_count, D).astype(jnp.bfloat16)
    placed = jnp.zeros((assign_count, D), jnp.bfloat16).at[order].set(outputs)
    return placed.reshape(PROMPT_TOKENS, TOP, D)

def reference(hidden, queries, keys, values, block_place, page_table, out_weight, norm_gain, gate_probs, routes, w_gate, w_up, w_down):
    every_row = jnp.arange(PROMPT_TOKENS, dtype=jnp.int32)
    positions = (block_place[every_row // HALF] * HALF + every_row % HALF).astype(jnp.int32)
    in_long = positions >= LONG
    rotary_position = positions - LONG * in_long.astype(jnp.int32)
    query_rotated = apply_rotary(queries, rotary_position, QUERY_HEADS)
    key_rotated = apply_rotary(keys, rotary_position, KEY_VALUE_HEADS)
    row_at = jnp.argsort(positions).astype(jnp.int32)
    logical = jnp.argsort(page_table).astype(jnp.int32)
    page_token_rows = row_at[(logical[:, None] * PAGE_TOKENS + jnp.arange(PAGE_TOKENS, dtype=jnp.int32)[None, :]).reshape(PAGE_TOTAL * PAGE_TOKENS)]
    key_value_pages = jnp.stack([key_rotated[page_token_rows], values[page_token_rows]], axis=1).reshape(PAGE_TOTAL, PAGE_TOKENS, 2, KEY_VALUE_HEADS * HEAD_SIZE)
    query_head_group = QUERY_HEADS // KEY_VALUE_HEADS
    score_scale = 1.0 / math.sqrt(HEAD_SIZE)
    keys_expanded = key_rotated.astype(jnp.float32).reshape(PROMPT_TOKENS, KEY_VALUE_HEADS, HEAD_SIZE)
    values_expanded = values.astype(jnp.float32).reshape(PROMPT_TOKENS, KEY_VALUE_HEADS, HEAD_SIZE)

    def attend(block_index):
        leading_row = block_index * TOKENS_PER_SEQ
        query_tile_block = lax.dynamic_slice_in_dim(query_rotated, leading_row, TOKENS_PER_SEQ).astype(jnp.float32).reshape(TOKENS_PER_SEQ, KEY_VALUE_HEADS, query_head_group, HEAD_SIZE)
        query_pos = lax.dynamic_slice_in_dim(positions, leading_row, TOKENS_PER_SEQ)
        scores = jnp.einsum('tkgd,nkd->kgtn', query_tile_block, keys_expanded) * score_scale
        allowed = ((query_pos >= LONG)[:, None] == in_long[None, :]) & (positions[None, :] <= query_pos[:, None])
        scores = jnp.where(allowed, scores, -1e+30)
        row_peak = lax.optimization_barrier(jnp.max(scores, axis=-1, keepdims=True))
        weights = jnp.where(allowed, jnp.exp(scores - row_peak), 0.0)
        row_total = lax.optimization_barrier(jnp.sum(weights, axis=-1))
        rounded = lax.optimization_barrier(weights.astype(jnp.bfloat16)).astype(jnp.float32)
        mixed = jnp.einsum('kgtn,nkd->kgtd', rounded, values_expanded) / row_total[..., None]
        return mixed.transpose(2, 0, 1, 3).reshape(TOKENS_PER_SEQ, QUERY_HEADS * HEAD_SIZE).astype(jnp.bfloat16)
    attended = lax.map(attend, jnp.arange(PROMPT_TOKENS // TOKENS_PER_SEQ, dtype=jnp.int32)).reshape(PROMPT_TOKENS, QUERY_HEADS * HEAD_SIZE)
    projected = jnp.dot(attended, out_weight, preferred_element_type=jnp.float32)
    residual = (hidden.astype(jnp.float32) + projected).astype(jnp.bfloat16)
    residual_wide = residual.astype(jnp.float32)
    mean_square = lax.optimization_barrier(jnp.mean(residual_wide * residual_wide, axis=-1, keepdims=True))
    normed = (residual_wide * lax.rsqrt(mean_square + EPS) * norm_gain).astype(jnp.bfloat16)
    chosen = expert_outputs(normed, routes, w_gate, w_up, w_down).astype(jnp.float32)
    gate_share = gate_probs / lax.optimization_barrier(jnp.sum(gate_probs, axis=1, keepdims=True))
    layer_out = (residual_wide + lax.optimization_barrier(jnp.sum(gate_share[:, :, None] * chosen, axis=1))).astype(jnp.bfloat16)
    return (layer_out, key_value_pages)
```

```python
import math

import jax
import jax.numpy as jnp
from jax import lax
from jax.sharding import PartitionSpec as P

HEAD_SIZE = 128
NEXP = 8
PAGE_TOKENS = 16
CHUNKS = 2


THETA = 1000000.0
EPS = 1e-05


def apply_rotary(values_in, positions, head_count):
    row_count = values_in.shape[0]
    split_view = values_in.astype(jnp.float32).reshape(row_count, head_count, HEAD_SIZE)
    steps_half = jnp.arange(HEAD_SIZE // 2, dtype=jnp.float32)
    frequency = THETA ** (-(2.0 * steps_half) / HEAD_SIZE)
    angles = positions.astype(jnp.float32)[:, None] * frequency[None, :]
    cosine = jnp.cos(angles)[:, None, :]
    sine_part = jnp.sin(angles)[:, None, :]
    front_half = split_view[..., : HEAD_SIZE // 2]
    back_half = split_view[..., HEAD_SIZE // 2 :]
    turned = jnp.concatenate(
        [front_half * cosine - back_half * sine_part, back_half * cosine + front_half * sine_part],
        axis=-1,
    )
    return turned.reshape(row_count, head_count * HEAD_SIZE).astype(jnp.bfloat16)


def per_device(
    hidden,
    queries,
    keys,
    values,
    block_place,
    page_table,
    out_weight,
    norm_gain,
    gate_probs,
    routes,
    w_gate,
    w_up,
    w_down,
):
    seq_count = lax.axis_size("seq")
    exp_count = lax.axis_size("exp")
    seq_index = lax.axis_index("seq")
    tok_rows = queries.shape[0]
    half_rows = tok_rows // 2
    all_rows = tok_rows * seq_count
    long_len = 3 * all_rows // 4
    all_pos = (
        block_place[:, None] * half_rows + jnp.arange(half_rows, dtype=jnp.int32)[None, :]
    ).reshape(all_rows)
    my_pos = lax.dynamic_slice_in_dim(all_pos, seq_index * tok_rows, tok_rows)
    my_long = my_pos >= long_len
    my_rope = my_pos - long_len * my_long.astype(jnp.int32)
    q_heads = queries.shape[1] // HEAD_SIZE
    kv_heads = keys.shape[1] // HEAD_SIZE
    query_head_group = q_heads // kv_heads
    query_rotated = apply_rotary(queries, my_rope, q_heads)
    key_rotated = apply_rotary(keys, my_rope, kv_heads)
    q_grid = query_rotated.reshape(tok_rows, kv_heads, query_head_group, HEAD_SIZE)
    score_scale = 1.0 / math.sqrt(HEAD_SIZE)
    page_count = tok_rows // PAGE_TOKENS
    page_total = page_table.shape[0]
    my_pages = seq_index * page_count + jnp.arange(page_count, dtype=jnp.int32)
    my_logical = jnp.sum(
        jnp.where(
            page_table[None, :] == my_pages[:, None],
            jnp.arange(page_total, dtype=jnp.int32)[None, :],
            0,
        ),
        axis=1,
    )
    block_count = block_place.shape[0]
    slot_of_block = jnp.sum(
        jnp.where(
            block_place[None, :] == jnp.arange(block_count, dtype=jnp.int32)[:, None],
            jnp.arange(block_count, dtype=jnp.int32)[None, :],
            0,
        ),
        axis=1,
    )
    wanted_pos = (
        my_logical[:, None] * PAGE_TOKENS + jnp.arange(PAGE_TOKENS, dtype=jnp.int32)[None, :]
    ).reshape(page_count * PAGE_TOKENS)
    taken = slot_of_block[wanted_pos // half_rows] * half_rows + wanted_pos % half_rows
    kv_width = key_rotated.shape[1]
    kv_all = lax.all_gather(
        jnp.concatenate([key_rotated, values], axis=1), "seq", axis=0, tiled=True
    )
    key_all, value_all = kv_all[:, :kv_width], kv_all[:, kv_width:]
    peak_old = jnp.full((kv_heads, query_head_group, tok_rows), -1e30, jnp.float32)
    row_count = key_all.shape[0]
    scores = (
        jnp.einsum(
            "tkgd,nkd->kgtn",
            q_grid,
            key_all.reshape(row_count, kv_heads, HEAD_SIZE),
            preferred_element_type=jnp.float32,
        )
        * score_scale
    )
    allowed = ((all_pos >= long_len)[None, :] == my_long[:, None]) & (
        all_pos[None, :] <= my_pos[:, None]
    )
    scores = jnp.where(allowed, scores, -1e30)
    peak_new = jnp.maximum(peak_old, jnp.max(scores, axis=-1))
    weights = jnp.where(allowed, jnp.exp(scores - peak_new[..., None]), 0.0)
    total_new = jnp.sum(weights, axis=-1)
    summed = jnp.einsum(
        "kgtn,nkd->kgtd",
        weights.astype(jnp.bfloat16),
        value_all.reshape(row_count, kv_heads, HEAD_SIZE),
        preferred_element_type=jnp.float32,
    )
    peak_final, total_final, summed = (peak_new, total_new, summed)
    cache_pages = jnp.stack([key_all[taken], value_all[taken]], axis=1).reshape(
        page_count, PAGE_TOKENS, 2, kv_heads * HEAD_SIZE
    )
    attended = (
        (summed / total_final[..., None])
        .transpose(2, 0, 1, 3)
        .reshape(tok_rows, q_heads * HEAD_SIZE)
        .astype(jnp.bfloat16)
    )
    partial_proj = jnp.dot(attended, out_weight, preferred_element_type=jnp.float32)
    projected = lax.psum_scatter(
        partial_proj.astype(jnp.bfloat16), "exp", scatter_dimension=1, tiled=True
    ).astype(jnp.float32)
    residual = (hidden.astype(jnp.float32) + projected).astype(jnp.bfloat16)
    top_count = routes.shape[1]
    capacity = tok_rows // 2
    assign_count = tok_rows * top_count
    flat_routes = routes.reshape(assign_count)
    expert_hot = (flat_routes[:, None] == jnp.arange(NEXP, dtype=jnp.int32)[None, :]).astype(
        jnp.float32
    )
    earlier = (jnp.arange(assign_count)[:, None] > jnp.arange(assign_count)[None, :]).astype(
        jnp.float32
    )
    before = jnp.dot(earlier, expert_hot, preferred_element_type=jnp.float32)
    slot_rank = jnp.sum(before * expert_hot, axis=1).astype(jnp.int32).reshape(tok_rows, top_count)
    slot_grid = routes * capacity + slot_rank
    chooser = jnp.any(
        slot_grid[None, :, :] == jnp.arange(NEXP * capacity, dtype=jnp.int32)[:, None, None],
        axis=-1,
    ).astype(jnp.bfloat16)
    outgoing_rows = jnp.dot(chooser, residual, preferred_element_type=jnp.float32).astype(
        jnp.bfloat16
    )
    expert_local = NEXP // exp_count
    arrived_rows = lax.all_to_all(
        outgoing_rows.reshape(exp_count, expert_local * capacity, -1),
        "exp",
        split_axis=0,
        concat_axis=2,
        tiled=True,
    )
    gathered_in = arrived_rows.astype(jnp.float32)
    mean_square = jnp.mean(gathered_in * gathered_in, axis=-1, keepdims=True)
    normed = (gathered_in * lax.rsqrt(mean_square + EPS) * norm_gain).astype(jnp.bfloat16)
    chunk_count = CHUNKS
    chunk_rows = capacity // chunk_count
    pieces = []
    for chunk in range(chunk_count):
        token_rows = lax.all_gather(
            normed[:, chunk * chunk_rows : (chunk + 1) * chunk_rows], "seq", axis=1, tiled=True
        )
        gate_part = jnp.einsum(
            "end,edf->enf", token_rows, w_gate, preferred_element_type=jnp.float32
        )
        up_part = jnp.einsum("end,edf->enf", token_rows, w_up, preferred_element_type=jnp.float32)
        hidden_units = (jax.nn.silu(gate_part) * up_part).astype(jnp.bfloat16)
        pieces.append(
            lax.psum_scatter(
                jnp.einsum(
                    "enf,efd->end", hidden_units, w_down, preferred_element_type=jnp.float32
                ).astype(jnp.bfloat16),
                "seq",
                scatter_dimension=1,
                tiled=True,
            )
        )
    returned = jnp.concatenate(pieces, axis=1)
    model_width = returned.shape[2]
    outbound = returned.reshape(capacity, exp_count, model_width // exp_count).transpose(1, 0, 2)
    homed = lax.all_to_all(outbound, "exp", split_axis=0, concat_axis=0, tiled=True)
    lookup = homed.reshape(NEXP * capacity, -1)
    chosen = (
        lookup[slot_grid.reshape(assign_count)]
        .astype(jnp.float32)
        .reshape(tok_rows, top_count, -1)
    )
    gate_share = gate_probs / jnp.sum(gate_probs, axis=1, keepdims=True)
    layer_out = (
        residual.astype(jnp.float32) + jnp.sum(gate_share[:, :, None] * chosen, axis=1)
    ).astype(jnp.bfloat16)
    return (layer_out, cache_pages)


def solution(mesh):
    return jax.shard_map(
        per_device,
        mesh=mesh,
        in_specs=(
            P("seq", "exp"),
            P("seq", "exp"),
            P("seq", "exp"),
            P("seq", "exp"),
            P(),
            P(),
            P("exp", None),
            P(),
            P("seq", None),
            P("seq", None),
            P("exp", None, "seq"),
            P("exp", None, "seq"),
            P("exp", "seq", None),
        ),
        out_specs=(P("seq", "exp"), P("seq", None, None, "exp")),
        check_vma=False,
    )
```

```python
import math

import jax
import jax.numpy as jnp
from jax import lax
from jax.sharding import PartitionSpec as P

HEAD_SIZE = 128
NEXP = 8
PAGE_TOKENS = 16


THETA = 1000000.0
EPS = 1e-05


def apply_rotary(values_in, positions, head_count):
    row_count = values_in.shape[0]
    split_view = values_in.astype(jnp.float32).reshape(row_count, head_count, HEAD_SIZE)
    steps_half = jnp.arange(HEAD_SIZE // 2, dtype=jnp.float32)
    frequency = THETA ** (-(2.0 * steps_half) / HEAD_SIZE)
    angles = positions.astype(jnp.float32)[:, None] * frequency[None, :]
    cosine = jnp.cos(angles)[:, None, :]
    sine_part = jnp.sin(angles)[:, None, :]
    front_half = split_view[..., : HEAD_SIZE // 2]
    back_half = split_view[..., HEAD_SIZE // 2 :]
    turned = jnp.concatenate(
        [front_half * cosine - back_half * sine_part, back_half * cosine + front_half * sine_part],
        axis=-1,
    )
    return turned.reshape(row_count, head_count * HEAD_SIZE).astype(jnp.bfloat16)


def shift_pairs(side, along, step):
    pairs = []
    for src in range(side * side):
        a, b = divmod(src, side)
        if along == 0:
            dst = ((a + step) % side) * side + b
        else:
            dst = a * side + (b + step) % side
        pairs.append((src, dst))
    return pairs


def ring_gather(piece, side, along):
    from_minus = lax.ppermute(piece, "seq", shift_pairs(side, along, 1))
    from_plus = lax.ppermute(piece, "seq", shift_pairs(side, along, -1))
    cut = piece.shape[-2] // 2
    far_a = lax.ppermute(from_minus[..., :cut, :], "seq", shift_pairs(side, along, 1))
    far_b = lax.ppermute(from_plus[..., cut:, :], "seq", shift_pairs(side, along, -1))
    far = jnp.concatenate([far_a, far_b], axis=-2)
    return [piece, from_plus, far, from_minus]


def gather_2d(piece_a, piece_b, side):
    a_rows = ring_gather(piece_a, side, 1)
    a_rows = ring_gather(jnp.stack(a_rows), side, 0)
    b_rows = ring_gather(piece_b, side, 0)
    b_rows = ring_gather(jnp.stack(b_rows), side, 1)
    return jnp.stack(a_rows), jnp.stack(b_rows, axis=1)


def ring_scatter(parts, side, along):
    cut = parts[0].shape[-2] // 2
    far = parts[2]
    got_m = lax.ppermute(far[..., :cut, :], "seq", shift_pairs(side, along, 1))
    got_p = lax.ppermute(far[..., cut:, :], "seq", shift_pairs(side, along, -1))
    near_p = parts[1].astype(jnp.float32)
    near_p = jnp.concatenate(
        [near_p[..., :cut, :] + got_m.astype(jnp.float32), near_p[..., cut:, :]], axis=-2
    )
    near_m = parts[3].astype(jnp.float32)
    near_m = jnp.concatenate(
        [near_m[..., :cut, :], near_m[..., cut:, :] + got_p.astype(jnp.float32)], axis=-2
    )
    recv_m = lax.ppermute(near_p.astype(jnp.bfloat16), "seq", shift_pairs(side, along, 1))
    recv_p = lax.ppermute(near_m.astype(jnp.bfloat16), "seq", shift_pairs(side, along, -1))
    return parts[0].astype(jnp.float32) + recv_m.astype(jnp.float32) + recv_p.astype(jnp.float32)


def scatter_2d(out_a, out_b, side):
    part_a = ring_scatter([out_a[k] for k in range(side)], side, 0).astype(jnp.bfloat16)
    part_a = ring_scatter([part_a[k] for k in range(side)], side, 1)
    part_b = ring_scatter([out_b[:, k] for k in range(side)], side, 1).astype(jnp.bfloat16)
    part_b = ring_scatter([part_b[k] for k in range(side)], side, 0)
    return part_a, part_b


def per_device(
    hidden,
    queries,
    keys,
    values,
    block_place,
    page_table,
    out_weight,
    norm_gain,
    gate_probs,
    routes,
    w_gate,
    w_up,
    w_down,
):
    seq_count = lax.axis_size("seq")
    exp_count = lax.axis_size("exp")
    seq_index = lax.axis_index("seq")
    tok_rows = queries.shape[0]
    half_rows = tok_rows // 2
    all_rows = tok_rows * seq_count
    long_len = 3 * all_rows // 4
    side = math.isqrt(seq_count)
    my_x, my_y = seq_index // side, seq_index % side
    offsets = jnp.arange(seq_count, dtype=jnp.int32)
    node_at = ((my_x + offsets // side) % side) * side + (my_y + offsets % side) % side
    halves_per_node = tok_rows // half_rows
    slot_at = (
        node_at[:, None] * halves_per_node + jnp.arange(halves_per_node, dtype=jnp.int32)[None, :]
    ).reshape(-1)
    block_count = block_place.shape[0]
    blocks_rel = jnp.sum(
        jnp.where(
            jnp.arange(block_count, dtype=jnp.int32)[None, :] == slot_at[:, None],
            block_place[None, :],
            0,
        ),
        axis=1,
    )
    all_pos = (
        blocks_rel[:, None] * half_rows + jnp.arange(half_rows, dtype=jnp.int32)[None, :]
    ).reshape(all_rows)
    my_pos = all_pos[:tok_rows]
    my_long = my_pos >= long_len
    my_rope = my_pos - long_len * my_long.astype(jnp.int32)
    q_heads = queries.shape[1] // HEAD_SIZE
    kv_heads = keys.shape[1] // HEAD_SIZE
    query_head_group = q_heads // kv_heads
    query_rotated = apply_rotary(queries, my_rope, q_heads)
    key_rotated = apply_rotary(keys, my_rope, kv_heads)
    q_grid = query_rotated.reshape(tok_rows, kv_heads, query_head_group, HEAD_SIZE)
    score_scale = 1.0 / math.sqrt(HEAD_SIZE)
    page_count = tok_rows // PAGE_TOKENS
    page_total = page_table.shape[0]
    my_pages = seq_index * page_count + jnp.arange(page_count, dtype=jnp.int32)
    my_logical = jnp.sum(
        jnp.where(
            page_table[None, :] == my_pages[:, None],
            jnp.arange(page_total, dtype=jnp.int32)[None, :],
            0,
        ),
        axis=1,
    )
    slot_of_block = jnp.sum(
        jnp.where(
            block_place[None, :] == jnp.arange(block_count, dtype=jnp.int32)[:, None],
            jnp.arange(block_count, dtype=jnp.int32)[None, :],
            0,
        ),
        axis=1,
    )
    wanted_pos = (
        my_logical[:, None] * PAGE_TOKENS + jnp.arange(PAGE_TOKENS, dtype=jnp.int32)[None, :]
    ).reshape(page_count * PAGE_TOKENS)
    taken_abs = slot_of_block[wanted_pos // half_rows] * half_rows + wanted_pos % half_rows
    taken_node = taken_abs // tok_rows
    taken = (
        (((taken_node // side - my_x) % side) * side + (taken_node % side - my_y) % side)
        * tok_rows
        + taken_abs % tok_rows
    )
    key_grid, value_grid = gather_2d(key_rotated, values, side)
    key_all = key_grid.reshape(all_rows, -1)
    value_all = value_grid.reshape(all_rows, -1)
    peak_old = jnp.full((kv_heads, query_head_group, tok_rows), -1e30, jnp.float32)
    row_count = key_all.shape[0]
    scores = (
        jnp.einsum(
            "tkgd,nkd->kgtn",
            q_grid,
            key_all.reshape(row_count, kv_heads, HEAD_SIZE),
            preferred_element_type=jnp.float32,
        )
        * score_scale
    )
    allowed = ((all_pos >= long_len)[None, :] == my_long[:, None]) & (
        all_pos[None, :] <= my_pos[:, None]
    )
    scores = jnp.where(allowed, scores, -1e30)
    peak_new = jnp.maximum(peak_old, jnp.max(scores, axis=-1))
    weights = jnp.where(allowed, jnp.exp(scores - peak_new[..., None]), 0.0)
    total_new = jnp.sum(weights, axis=-1)
    summed = jnp.einsum(
        "kgtn,nkd->kgtd",
        weights.astype(jnp.bfloat16),
        value_all.reshape(row_count, kv_heads, HEAD_SIZE),
        preferred_element_type=jnp.float32,
    )
    peak_final, total_final, summed = (peak_new, total_new, summed)
    cache_pages = jnp.stack([key_all[taken], value_all[taken]], axis=1).reshape(
        page_count, PAGE_TOKENS, 2, kv_heads * HEAD_SIZE
    )
    attended = (
        (summed / total_final[..., None])
        .transpose(2, 0, 1, 3)
        .reshape(tok_rows, q_heads * HEAD_SIZE)
        .astype(jnp.bfloat16)
    )
    partial_proj = jnp.dot(attended, out_weight, preferred_element_type=jnp.float32)
    projected = lax.psum_scatter(
        partial_proj.astype(jnp.bfloat16), "exp", scatter_dimension=1, tiled=True
    ).astype(jnp.float32)
    residual = (hidden.astype(jnp.float32) + projected).astype(jnp.bfloat16)
    top_count = routes.shape[1]
    capacity = tok_rows // 2
    assign_count = tok_rows * top_count
    flat_routes = routes.reshape(assign_count)
    expert_hot = (flat_routes[:, None] == jnp.arange(NEXP, dtype=jnp.int32)[None, :]).astype(
        jnp.float32
    )
    earlier = (jnp.arange(assign_count)[:, None] > jnp.arange(assign_count)[None, :]).astype(
        jnp.float32
    )
    before = jnp.dot(earlier, expert_hot, preferred_element_type=jnp.float32)
    slot_rank = jnp.sum(before * expert_hot, axis=1).astype(jnp.int32).reshape(tok_rows, top_count)
    slot_grid = routes * capacity + slot_rank
    chooser = jnp.any(
        slot_grid[None, :, :] == jnp.arange(NEXP * capacity, dtype=jnp.int32)[:, None, None],
        axis=-1,
    ).astype(jnp.bfloat16)
    outgoing_rows = jnp.dot(chooser, residual, preferred_element_type=jnp.float32).astype(
        jnp.bfloat16
    )
    expert_local = NEXP // exp_count
    arrived_rows = lax.all_to_all(
        outgoing_rows.reshape(exp_count, expert_local * capacity, -1),
        "exp",
        split_axis=0,
        concat_axis=2,
        tiled=True,
    )
    gathered_in = arrived_rows.astype(jnp.float32)
    mean_square = jnp.mean(gathered_in * gathered_in, axis=-1, keepdims=True)
    normed = (gathered_in * lax.rsqrt(mean_square + EPS) * norm_gain).astype(jnp.bfloat16)
    rows_in = normed[0]
    model_width = rows_in.shape[1]
    cut = model_width // 2
    grid_a, grid_b = gather_2d(rows_in[:, :cut], rows_in[:, cut:], side)
    rows_a = grid_a.reshape(-1, cut)
    rows_b = grid_b.reshape(-1, cut)
    gate_part = jnp.dot(rows_a, w_gate[0, :cut], preferred_element_type=jnp.float32) + jnp.dot(
        rows_b, w_gate[0, cut:], preferred_element_type=jnp.float32
    )
    up_part = jnp.dot(rows_a, w_up[0, :cut], preferred_element_type=jnp.float32) + jnp.dot(
        rows_b, w_up[0, cut:], preferred_element_type=jnp.float32
    )
    hidden_units = (jax.nn.silu(gate_part) * up_part).astype(jnp.bfloat16)
    grid_shape = (side, side, capacity, cut)
    out_a = jnp.dot(hidden_units, w_down[0, :, :cut], preferred_element_type=jnp.float32)
    out_b = jnp.dot(hidden_units, w_down[0, :, cut:], preferred_element_type=jnp.float32)
    part_a, part_b = scatter_2d(
        out_a.astype(jnp.bfloat16).reshape(grid_shape),
        out_b.astype(jnp.bfloat16).reshape(grid_shape),
        side,
    )
    returned = jnp.concatenate([part_a, part_b], axis=1).astype(jnp.bfloat16)
    outbound = returned.reshape(capacity, exp_count, model_width // exp_count).transpose(1, 0, 2)
    homed = lax.all_to_all(outbound, "exp", split_axis=0, concat_axis=0, tiled=True)
    lookup = homed.reshape(NEXP * capacity, -1)
    chosen = (
        lookup[slot_grid.reshape(assign_count)]
        .astype(jnp.float32)
        .reshape(tok_rows, top_count, -1)
    )
    gate_share = gate_probs / jnp.sum(gate_probs, axis=1, keepdims=True)
    layer_out = (
        residual.astype(jnp.float32) + jnp.sum(gate_share[:, :, None] * chosen, axis=1)
    ).astype(jnp.bfloat16)
    return (layer_out, cache_pages)


def solution(mesh):
    return jax.shard_map(
        per_device,
        mesh=mesh,
        in_specs=(
            P("seq", "exp"),
            P("seq", "exp"),
            P("seq", "exp"),
            P("seq", "exp"),
            P(),
            P(),
            P("exp", None),
            P(),
            P("seq", None),
            P("seq", None),
            P("exp", None, "seq"),
            P("exp", None, "seq"),
            P("exp", "seq", None),
        ),
        out_specs=(P("seq", "exp"), P("seq", None, None, "exp")),
        check_vma=False,
    )
```

```python
import math

import jax
import jax.numpy as jnp
from jax import lax
from jax.sharding import PartitionSpec as P

HEAD_SIZE = 128
NEXP = 8
PAGE_TOKENS = 16


THETA = 1000000.0
EPS = 1e-05


def apply_rotary(values_in, positions, head_count):
    row_count = values_in.shape[0]
    split_view = values_in.astype(jnp.float32).reshape(row_count, head_count, HEAD_SIZE)
    steps_half = jnp.arange(HEAD_SIZE // 2, dtype=jnp.float32)
    frequency = THETA ** (-(2.0 * steps_half) / HEAD_SIZE)
    angles = positions.astype(jnp.float32)[:, None] * frequency[None, :]
    cosine = jnp.cos(angles)[:, None, :]
    sine_part = jnp.sin(angles)[:, None, :]
    front_half = split_view[..., : HEAD_SIZE // 2]
    back_half = split_view[..., HEAD_SIZE // 2 :]
    turned = jnp.concatenate(
        [front_half * cosine - back_half * sine_part, back_half * cosine + front_half * sine_part],
        axis=-1,
    )
    return turned.reshape(row_count, head_count * HEAD_SIZE).astype(jnp.bfloat16)


def shift_pairs(side, along, step):
    pairs = []
    for src in range(side * side):
        a, b = divmod(src, side)
        if along == 0:
            dst = ((a + step) % side) * side + b
        else:
            dst = a * side + (b + step) % side
        pairs.append((src, dst))
    return pairs


def ring_gather_whole(piece, perm_of):
    from_minus = lax.ppermute(piece, "seq", perm_of(1))
    from_plus = lax.ppermute(piece, "seq", perm_of(-1))
    far = lax.ppermute(from_minus, "seq", perm_of(1))
    return [piece, from_plus, far, from_minus]


def exp_ring_pairs(zside, step):
    pairs = []
    for src in range(zside * 2):
        z, core = divmod(src, 2)
        pairs.append((src, ((z + step) % zside) * 2 + core))
    return pairs


def scatter_exp(partial, exp_count):
    rows, width = partial.shape
    zside = exp_count // 2
    block = width // exp_count
    exp_index = lax.axis_index("exp")
    my_z, my_core = exp_index // 2, exp_index % 2
    grid = partial.astype(jnp.bfloat16).reshape(rows, zside, 2, block)
    mine = lax.dynamic_index_in_dim(grid, my_core, axis=2, keepdims=False)
    theirs = lax.dynamic_index_in_dim(grid, 1 - my_core, axis=2, keepdims=False)
    swapped = lax.ppermute(theirs, "exp", [(e, e ^ 1) for e in range(exp_count)])
    chip_sum = (mine.astype(jnp.float32) + swapped.astype(jnp.float32)).astype(jnp.bfloat16)
    parts = [
        lax.dynamic_index_in_dim(chip_sum, (my_z + k) % zside, axis=1, keepdims=False)
        for k in range(zside)
    ]
    cut = rows // 2
    far = parts[2]
    got_m = lax.ppermute(far[:cut], "exp", exp_ring_pairs(zside, 1))
    got_p = lax.ppermute(far[cut:], "exp", exp_ring_pairs(zside, -1))
    near_p = parts[1].astype(jnp.float32)
    near_p = jnp.concatenate([near_p[:cut] + got_m.astype(jnp.float32), near_p[cut:]], axis=0)
    near_m = parts[3].astype(jnp.float32)
    near_m = jnp.concatenate([near_m[:cut], near_m[cut:] + got_p.astype(jnp.float32)], axis=0)
    recv_m = lax.ppermute(near_p.astype(jnp.bfloat16), "exp", exp_ring_pairs(zside, 1))
    recv_p = lax.ppermute(near_m.astype(jnp.bfloat16), "exp", exp_ring_pairs(zside, -1))
    return parts[0].astype(jnp.float32) + recv_m.astype(jnp.float32) + recv_p.astype(jnp.float32)


def ring_gather(piece, side, along):
    from_minus = lax.ppermute(piece, "seq", shift_pairs(side, along, 1))
    from_plus = lax.ppermute(piece, "seq", shift_pairs(side, along, -1))
    cut = piece.shape[-2] // 2
    far_a = lax.ppermute(from_minus[..., :cut, :], "seq", shift_pairs(side, along, 1))
    far_b = lax.ppermute(from_plus[..., cut:, :], "seq", shift_pairs(side, along, -1))
    far = jnp.concatenate([far_a, far_b], axis=-2)
    return [piece, from_plus, far, from_minus]


def gather_2d(piece_a, piece_b, side):
    a_rows = ring_gather(piece_a, side, 1)
    a_rows = ring_gather(jnp.stack(a_rows), side, 0)
    b_rows = ring_gather(piece_b, side, 0)
    b_rows = ring_gather(jnp.stack(b_rows), side, 1)
    return jnp.stack(a_rows), jnp.stack(b_rows, axis=1)


def ring_scatter(parts, side, along):
    cut = parts[0].shape[-2] // 2
    far = parts[2]
    got_m = lax.ppermute(far[..., :cut, :], "seq", shift_pairs(side, along, 1))
    got_p = lax.ppermute(far[..., cut:, :], "seq", shift_pairs(side, along, -1))
    near_p = parts[1].astype(jnp.float32)
    near_p = jnp.concatenate(
        [near_p[..., :cut, :] + got_m.astype(jnp.float32), near_p[..., cut:, :]], axis=-2
    )
    near_m = parts[3].astype(jnp.float32)
    near_m = jnp.concatenate(
        [near_m[..., :cut, :], near_m[..., cut:, :] + got_p.astype(jnp.float32)], axis=-2
    )
    recv_m = lax.ppermute(near_p.astype(jnp.bfloat16), "seq", shift_pairs(side, along, 1))
    recv_p = lax.ppermute(near_m.astype(jnp.bfloat16), "seq", shift_pairs(side, along, -1))
    return parts[0].astype(jnp.float32) + recv_m.astype(jnp.float32) + recv_p.astype(jnp.float32)


def scatter_2d(out_a, out_b, side):
    part_a = ring_scatter([out_a[k] for k in range(side)], side, 0).astype(jnp.bfloat16)
    part_a = ring_scatter([part_a[k] for k in range(side)], side, 1)
    part_b = ring_scatter([out_b[:, k] for k in range(side)], side, 1).astype(jnp.bfloat16)
    part_b = ring_scatter([part_b[k] for k in range(side)], side, 0)
    return part_a, part_b


def per_device(
    hidden,
    queries,
    keys,
    values,
    block_place,
    page_table,
    out_weight,
    norm_gain,
    gate_probs,
    routes,
    w_gate,
    w_up,
    w_down,
):
    seq_count = lax.axis_size("seq")
    exp_count = lax.axis_size("exp")
    seq_index = lax.axis_index("seq")
    tok_rows = queries.shape[0]
    half_rows = tok_rows // 2
    all_rows = tok_rows * seq_count
    long_len = 3 * all_rows // 4
    side = math.isqrt(seq_count)
    my_x, my_y = seq_index // side, seq_index % side
    offsets = jnp.arange(seq_count, dtype=jnp.int32)
    node_at = ((my_x + offsets // side) % side) * side + (my_y + offsets % side) % side
    halves_per_node = tok_rows // half_rows
    slot_at = (
        node_at[:, None] * halves_per_node + jnp.arange(halves_per_node, dtype=jnp.int32)[None, :]
    ).reshape(-1)
    block_count = block_place.shape[0]
    blocks_rel = jnp.sum(
        jnp.where(
            jnp.arange(block_count, dtype=jnp.int32)[None, :] == slot_at[:, None],
            block_place[None, :],
            0,
        ),
        axis=1,
    )
    all_pos = (
        blocks_rel[:, None] * half_rows + jnp.arange(half_rows, dtype=jnp.int32)[None, :]
    ).reshape(all_rows)
    my_pos = all_pos[:tok_rows]
    my_long = my_pos >= long_len
    my_rope = my_pos - long_len * my_long.astype(jnp.int32)
    q_heads = queries.shape[1] // HEAD_SIZE
    kv_heads = keys.shape[1] // HEAD_SIZE
    query_head_group = q_heads // kv_heads
    query_rotated = apply_rotary(queries, my_rope, q_heads)
    key_rotated = apply_rotary(keys, my_rope, kv_heads)
    q_grid = query_rotated.reshape(tok_rows, kv_heads, query_head_group, HEAD_SIZE)
    score_scale = 1.0 / math.sqrt(HEAD_SIZE)
    page_count = tok_rows // PAGE_TOKENS
    page_total = page_table.shape[0]
    my_pages = seq_index * page_count + jnp.arange(page_count, dtype=jnp.int32)
    my_logical = jnp.sum(
        jnp.where(
            page_table[None, :] == my_pages[:, None],
            jnp.arange(page_total, dtype=jnp.int32)[None, :],
            0,
        ),
        axis=1,
    )
    slot_of_block = jnp.sum(
        jnp.where(
            block_place[None, :] == jnp.arange(block_count, dtype=jnp.int32)[:, None],
            jnp.arange(block_count, dtype=jnp.int32)[None, :],
            0,
        ),
        axis=1,
    )
    wanted_pos = (
        my_logical[:, None] * PAGE_TOKENS + jnp.arange(PAGE_TOKENS, dtype=jnp.int32)[None, :]
    ).reshape(page_count * PAGE_TOKENS)
    taken_abs = slot_of_block[wanted_pos // half_rows] * half_rows + wanted_pos % half_rows
    taken_node = taken_abs // tok_rows
    taken = (
        (((taken_node // side - my_x) % side) * side + (taken_node % side - my_y) % side)
        * tok_rows
        + taken_abs % tok_rows
    )
    kv_width = key_rotated.shape[1]
    kv_rows = ring_gather_whole(
        jnp.concatenate([key_rotated, values], axis=1), lambda step: shift_pairs(side, 1, step)
    )
    kv_rows = ring_gather_whole(jnp.stack(kv_rows), lambda step: shift_pairs(side, 0, step))
    kv_all = jnp.stack(kv_rows).reshape(all_rows, 2 * kv_width)
    key_all, value_all = kv_all[:, :kv_width], kv_all[:, kv_width:]
    peak_old = jnp.full((kv_heads, query_head_group, tok_rows), -1e30, jnp.float32)
    row_count = key_all.shape[0]
    scores = (
        jnp.einsum(
            "tkgd,nkd->kgtn",
            q_grid,
            key_all.reshape(row_count, kv_heads, HEAD_SIZE),
            preferred_element_type=jnp.float32,
        )
        * score_scale
    )
    allowed = ((all_pos >= long_len)[None, :] == my_long[:, None]) & (
        all_pos[None, :] <= my_pos[:, None]
    )
    scores = jnp.where(allowed, scores, -1e30)
    peak_new = jnp.maximum(peak_old, jnp.max(scores, axis=-1))
    weights = jnp.where(allowed, jnp.exp(scores - peak_new[..., None]), 0.0)
    total_new = jnp.sum(weights, axis=-1)
    summed = jnp.einsum(
        "kgtn,nkd->kgtd",
        weights.astype(jnp.bfloat16),
        value_all.reshape(row_count, kv_heads, HEAD_SIZE),
        preferred_element_type=jnp.float32,
    )
    peak_final, total_final, summed = (peak_new, total_new, summed)
    cache_pages = jnp.stack([key_all[taken], value_all[taken]], axis=1).reshape(
        page_count, PAGE_TOKENS, 2, kv_heads * HEAD_SIZE
    )
    attended = (
        (summed / total_final[..., None])
        .transpose(2, 0, 1, 3)
        .reshape(tok_rows, q_heads * HEAD_SIZE)
        .astype(jnp.bfloat16)
    )
    partial_proj = jnp.dot(attended, out_weight, preferred_element_type=jnp.float32)
    projected = scatter_exp(partial_proj, exp_count)
    residual = (hidden.astype(jnp.float32) + projected).astype(jnp.bfloat16)
    top_count = routes.shape[1]
    capacity = tok_rows // 2
    assign_count = tok_rows * top_count
    flat_routes = routes.reshape(assign_count)
    expert_hot = (flat_routes[:, None] == jnp.arange(NEXP, dtype=jnp.int32)[None, :]).astype(
        jnp.float32
    )
    earlier = (jnp.arange(assign_count)[:, None] > jnp.arange(assign_count)[None, :]).astype(
        jnp.float32
    )
    before = jnp.dot(earlier, expert_hot, preferred_element_type=jnp.float32)
    slot_rank = jnp.sum(before * expert_hot, axis=1).astype(jnp.int32).reshape(tok_rows, top_count)
    slot_grid = routes * capacity + slot_rank
    chooser = jnp.any(
        slot_grid[None, :, :] == jnp.arange(NEXP * capacity, dtype=jnp.int32)[:, None, None],
        axis=-1,
    ).astype(jnp.bfloat16)
    outgoing_rows = jnp.dot(chooser, residual, preferred_element_type=jnp.float32).astype(
        jnp.bfloat16
    )
    expert_local = NEXP // exp_count
    arrived_rows = lax.all_to_all(
        outgoing_rows.reshape(exp_count, expert_local * capacity, -1),
        "exp",
        split_axis=0,
        concat_axis=2,
        tiled=True,
    )
    gathered_in = arrived_rows.astype(jnp.float32)
    mean_square = jnp.mean(gathered_in * gathered_in, axis=-1, keepdims=True)
    normed = (gathered_in * lax.rsqrt(mean_square + EPS) * norm_gain).astype(jnp.bfloat16)
    rows_in = normed[0]
    model_width = rows_in.shape[1]
    cut = model_width // 2
    grid_a, grid_b = gather_2d(rows_in[:, :cut], rows_in[:, cut:], side)
    rows_a = grid_a.reshape(-1, cut)
    rows_b = grid_b.reshape(-1, cut)
    gate_part = jnp.dot(rows_a, w_gate[0, :cut], preferred_element_type=jnp.float32) + jnp.dot(
        rows_b, w_gate[0, cut:], preferred_element_type=jnp.float32
    )
    up_part = jnp.dot(rows_a, w_up[0, :cut], preferred_element_type=jnp.float32) + jnp.dot(
        rows_b, w_up[0, cut:], preferred_element_type=jnp.float32
    )
    hidden_units = (jax.nn.silu(gate_part) * up_part).astype(jnp.bfloat16)
    grid_shape = (side, side, capacity, cut)
    out_a = jnp.dot(hidden_units, w_down[0, :, :cut], preferred_element_type=jnp.float32)
    out_b = jnp.dot(hidden_units, w_down[0, :, cut:], preferred_element_type=jnp.float32)
    part_a, part_b = scatter_2d(
        out_a.astype(jnp.bfloat16).reshape(grid_shape),
        out_b.astype(jnp.bfloat16).reshape(grid_shape),
        side,
    )
    returned = jnp.concatenate([part_a, part_b], axis=1).astype(jnp.bfloat16)
    outbound = returned.reshape(capacity, exp_count, model_width // exp_count).transpose(1, 0, 2)
    homed = lax.all_to_all(outbound, "exp", split_axis=0, concat_axis=0, tiled=True)
    lookup = homed.reshape(NEXP * capacity, -1)
    chosen = (
        lookup[slot_grid.reshape(assign_count)]
        .astype(jnp.float32)
        .reshape(tok_rows, top_count, -1)
    )
    gate_share = gate_probs / jnp.sum(gate_probs, axis=1, keepdims=True)
    layer_out = (
        residual.astype(jnp.float32) + jnp.sum(gate_share[:, :, None] * chosen, axis=1)
    ).astype(jnp.bfloat16)
    return (layer_out, cache_pages)


def solution(mesh):
    return jax.shard_map(
        per_device,
        mesh=mesh,
        in_specs=(
            P("seq", "exp"),
            P("seq", "exp"),
            P("seq", "exp"),
            P("seq", "exp"),
            P(),
            P(),
            P("exp", None),
            P(),
            P("seq", None),
            P("seq", None),
            P("exp", None, "seq"),
            P("exp", None, "seq"),
            P("exp", "seq", None),
        ),
        out_specs=(P("seq", "exp"), P("seq", None, None, "exp")),
        check_vma=False,
    )
```

```python
import math

import jax
import jax.numpy as jnp
from jax import lax
from jax.sharding import PartitionSpec as P

HEAD_SIZE = 128
NEXP = 8
PAGE_TOKENS = 16


THETA = 1000000.0
EPS = 1e-05


def apply_rotary(values_in, positions, head_count):
    row_count = values_in.shape[0]
    split_view = values_in.astype(jnp.float32).reshape(row_count, head_count, HEAD_SIZE)
    steps_half = jnp.arange(HEAD_SIZE // 2, dtype=jnp.float32)
    frequency = THETA ** (-(2.0 * steps_half) / HEAD_SIZE)
    angles = positions.astype(jnp.float32)[:, None] * frequency[None, :]
    cosine = jnp.cos(angles)[:, None, :]
    sine_part = jnp.sin(angles)[:, None, :]
    front_half = split_view[..., : HEAD_SIZE // 2]
    back_half = split_view[..., HEAD_SIZE // 2 :]
    turned = jnp.concatenate(
        [front_half * cosine - back_half * sine_part, back_half * cosine + front_half * sine_part],
        axis=-1,
    )
    return turned.reshape(row_count, head_count * HEAD_SIZE).astype(jnp.bfloat16)


def shift_pairs(side, along, step):
    pairs = []
    for src in range(side * side):
        a, b = divmod(src, side)
        if along == 0:
            dst = ((a + step) % side) * side + b
        else:
            dst = a * side + (b + step) % side
        pairs.append((src, dst))
    return pairs


def ring_gather_whole(piece, perm_of):
    from_minus = lax.ppermute(piece, "seq", perm_of(1))
    from_plus = lax.ppermute(piece, "seq", perm_of(-1))
    far = lax.ppermute(from_minus, "seq", perm_of(1))
    return [piece, from_plus, far, from_minus]


def exp_ring_pairs(zside, step):
    pairs = []
    for src in range(zside * 2):
        z, core = divmod(src, 2)
        pairs.append((src, ((z + step) % zside) * 2 + core))
    return pairs


def scatter_exp(partial, exp_count):
    rows, width = partial.shape
    zside = exp_count // 2
    block = width // exp_count
    exp_index = lax.axis_index("exp")
    my_z, my_core = exp_index // 2, exp_index % 2
    grid = partial.astype(jnp.bfloat16).reshape(rows, zside, 2, block)
    mine = lax.dynamic_index_in_dim(grid, my_core, axis=2, keepdims=False)
    theirs = lax.dynamic_index_in_dim(grid, 1 - my_core, axis=2, keepdims=False)
    swapped = lax.ppermute(theirs, "exp", [(e, e ^ 1) for e in range(exp_count)])
    chip_sum = (mine.astype(jnp.float32) + swapped.astype(jnp.float32)).astype(jnp.bfloat16)
    parts = [
        lax.dynamic_index_in_dim(chip_sum, (my_z + k) % zside, axis=1, keepdims=False)
        for k in range(zside)
    ]
    cut = rows // 2
    far = parts[2]
    got_m = lax.ppermute(far[:cut], "exp", exp_ring_pairs(zside, 1))
    got_p = lax.ppermute(far[cut:], "exp", exp_ring_pairs(zside, -1))
    near_p = parts[1].astype(jnp.float32)
    near_p = jnp.concatenate([near_p[:cut] + got_m.astype(jnp.float32), near_p[cut:]], axis=0)
    near_m = parts[3].astype(jnp.float32)
    near_m = jnp.concatenate([near_m[:cut], near_m[cut:] + got_p.astype(jnp.float32)], axis=0)
    recv_m = lax.ppermute(near_p.astype(jnp.bfloat16), "exp", exp_ring_pairs(zside, 1))
    recv_p = lax.ppermute(near_m.astype(jnp.bfloat16), "exp", exp_ring_pairs(zside, -1))
    return parts[0].astype(jnp.float32) + recv_m.astype(jnp.float32) + recv_p.astype(jnp.float32)


def ring_gather(piece, side, along):
    from_minus = lax.ppermute(piece, "seq", shift_pairs(side, along, 1))
    from_plus = lax.ppermute(piece, "seq", shift_pairs(side, along, -1))
    cut = piece.shape[-2] // 2
    far_a = lax.ppermute(from_minus[..., :cut, :], "seq", shift_pairs(side, along, 1))
    far_b = lax.ppermute(from_plus[..., cut:, :], "seq", shift_pairs(side, along, -1))
    far = jnp.concatenate([far_a, far_b], axis=-2)
    return [piece, from_plus, far, from_minus]


def gather_2d(piece_a, piece_b, side):
    a_rows = ring_gather(piece_a, side, 1)
    a_rows = ring_gather(jnp.stack(a_rows), side, 0)
    b_rows = ring_gather(piece_b, side, 0)
    b_rows = ring_gather(jnp.stack(b_rows), side, 1)
    return jnp.stack(a_rows), jnp.stack(b_rows, axis=1)


def ring_scatter(parts, side, along):
    cut = parts[0].shape[-2] // 2
    far = parts[2]
    got_m = lax.ppermute(far[..., :cut, :], "seq", shift_pairs(side, along, 1))
    got_p = lax.ppermute(far[..., cut:, :], "seq", shift_pairs(side, along, -1))
    near_p = parts[1].astype(jnp.float32)
    near_p = jnp.concatenate(
        [near_p[..., :cut, :] + got_m.astype(jnp.float32), near_p[..., cut:, :]], axis=-2
    )
    near_m = parts[3].astype(jnp.float32)
    near_m = jnp.concatenate(
        [near_m[..., :cut, :], near_m[..., cut:, :] + got_p.astype(jnp.float32)], axis=-2
    )
    recv_m = lax.ppermute(near_p.astype(jnp.bfloat16), "seq", shift_pairs(side, along, 1))
    recv_p = lax.ppermute(near_m.astype(jnp.bfloat16), "seq", shift_pairs(side, along, -1))
    return parts[0].astype(jnp.float32) + recv_m.astype(jnp.float32) + recv_p.astype(jnp.float32)


def scatter_2d(out_a, out_b, side):
    part_a = ring_scatter([out_a[k] for k in range(side)], side, 0).astype(jnp.bfloat16)
    part_a = ring_scatter([part_a[k] for k in range(side)], side, 1)
    part_b = ring_scatter([out_b[:, k] for k in range(side)], side, 1).astype(jnp.bfloat16)
    part_b = ring_scatter([part_b[k] for k in range(side)], side, 0)
    return part_a, part_b


def per_device(
    hidden,
    queries,
    keys,
    values,
    block_place,
    page_table,
    out_weight,
    norm_gain,
    gate_probs,
    routes,
    w_gate,
    w_up,
    w_down,
):
    seq_count = lax.axis_size("seq")
    exp_count = lax.axis_size("exp")
    seq_index = lax.axis_index("seq")
    tok_rows = queries.shape[0]
    half_rows = tok_rows // 2
    all_rows = tok_rows * seq_count
    long_len = 3 * all_rows // 4
    side = math.isqrt(seq_count)
    my_x, my_y = seq_index // side, seq_index % side
    block_count = block_place.shape[0]
    all_pos = (
        block_place[:, None] * half_rows + jnp.arange(half_rows, dtype=jnp.int32)[None, :]
    ).reshape(all_rows)
    my_pos = lax.dynamic_slice_in_dim(all_pos, seq_index * tok_rows, tok_rows)
    my_long = my_pos >= long_len
    my_rope = my_pos - long_len * my_long.astype(jnp.int32)
    q_heads = queries.shape[1] // HEAD_SIZE
    kv_heads = keys.shape[1] // HEAD_SIZE
    query_head_group = q_heads // kv_heads
    query_rotated = apply_rotary(queries, my_rope, q_heads)
    key_rotated = apply_rotary(keys, my_rope, kv_heads)
    q_grid = query_rotated.reshape(tok_rows, kv_heads, query_head_group, HEAD_SIZE)
    score_scale = 1.0 / math.sqrt(HEAD_SIZE)
    page_count = tok_rows // PAGE_TOKENS
    page_total = page_table.shape[0]
    my_pages = seq_index * page_count + jnp.arange(page_count, dtype=jnp.int32)
    my_logical = jnp.sum(
        jnp.where(
            page_table[None, :] == my_pages[:, None],
            jnp.arange(page_total, dtype=jnp.int32)[None, :],
            0,
        ),
        axis=1,
    )
    slot_of_block = jnp.sum(
        jnp.where(
            block_place[None, :] == jnp.arange(block_count, dtype=jnp.int32)[:, None],
            jnp.arange(block_count, dtype=jnp.int32)[None, :],
            0,
        ),
        axis=1,
    )
    wanted_pos = (
        my_logical[:, None] * PAGE_TOKENS + jnp.arange(PAGE_TOKENS, dtype=jnp.int32)[None, :]
    ).reshape(page_count * PAGE_TOKENS)
    taken_abs = slot_of_block[wanted_pos // half_rows] * half_rows + wanted_pos % half_rows
    taken = taken_abs
    kv_width = key_rotated.shape[1]
    kv_piece = jnp.concatenate([key_rotated, values], axis=1)
    kv_all = lax.all_to_all(
        jnp.broadcast_to(kv_piece[None], (seq_count,) + kv_piece.shape),
        "seq",
        split_axis=0,
        concat_axis=0,
        tiled=True,
    ).reshape(all_rows, 2 * kv_width)
    key_all, value_all = kv_all[:, :kv_width], kv_all[:, kv_width:]
    peak_old = jnp.full((kv_heads, query_head_group, tok_rows), -1e30, jnp.float32)
    row_count = key_all.shape[0]
    scores = (
        jnp.einsum(
            "tkgd,nkd->kgtn",
            q_grid,
            key_all.reshape(row_count, kv_heads, HEAD_SIZE),
            preferred_element_type=jnp.float32,
        )
        * score_scale
    )
    allowed = ((all_pos >= long_len)[None, :] == my_long[:, None]) & (
        all_pos[None, :] <= my_pos[:, None]
    )
    scores = jnp.where(allowed, scores, -1e30)
    peak_new = jnp.maximum(peak_old, jnp.max(scores, axis=-1))
    weights = jnp.where(allowed, jnp.exp(scores - peak_new[..., None]), 0.0)
    total_new = jnp.sum(weights, axis=-1)
    summed = jnp.einsum(
        "kgtn,nkd->kgtd",
        weights.astype(jnp.bfloat16),
        value_all.reshape(row_count, kv_heads, HEAD_SIZE),
        preferred_element_type=jnp.float32,
    )
    peak_final, total_final, summed = (peak_new, total_new, summed)
    cache_pages = jnp.stack([key_all[taken], value_all[taken]], axis=1).reshape(
        page_count, PAGE_TOKENS, 2, kv_heads * HEAD_SIZE
    )
    attended = (
        (summed / total_final[..., None])
        .transpose(2, 0, 1, 3)
        .reshape(tok_rows, q_heads * HEAD_SIZE)
        .astype(jnp.bfloat16)
    )
    partial_proj = jnp.dot(attended, out_weight, preferred_element_type=jnp.float32)
    projected = scatter_exp(partial_proj, exp_count)
    residual = (hidden.astype(jnp.float32) + projected).astype(jnp.bfloat16)
    top_count = routes.shape[1]
    capacity = tok_rows // 2
    assign_count = tok_rows * top_count
    flat_routes = routes.reshape(assign_count)
    expert_hot = (flat_routes[:, None] == jnp.arange(NEXP, dtype=jnp.int32)[None, :]).astype(
        jnp.float32
    )
    earlier = (jnp.arange(assign_count)[:, None] > jnp.arange(assign_count)[None, :]).astype(
        jnp.float32
    )
    before = jnp.dot(earlier, expert_hot, preferred_element_type=jnp.float32)
    slot_rank = jnp.sum(before * expert_hot, axis=1).astype(jnp.int32).reshape(tok_rows, top_count)
    slot_grid = routes * capacity + slot_rank
    chooser = jnp.any(
        slot_grid[None, :, :] == jnp.arange(NEXP * capacity, dtype=jnp.int32)[:, None, None],
        axis=-1,
    ).astype(jnp.bfloat16)
    outgoing_rows = jnp.dot(chooser, residual, preferred_element_type=jnp.float32).astype(
        jnp.bfloat16
    )
    expert_local = NEXP // exp_count
    arrived_rows = lax.all_to_all(
        outgoing_rows.reshape(exp_count, expert_local * capacity, -1),
        "exp",
        split_axis=0,
        concat_axis=2,
        tiled=True,
    )
    gathered_in = arrived_rows.astype(jnp.float32)
    mean_square = jnp.mean(gathered_in * gathered_in, axis=-1, keepdims=True)
    normed = (gathered_in * lax.rsqrt(mean_square + EPS) * norm_gain).astype(jnp.bfloat16)
    rows_in = normed[0]
    model_width = rows_in.shape[1]
    cut = model_width // 2
    a_rows = ring_gather(rows_in[:, :cut], side, 1)
    a_rows = ring_gather(jnp.stack(a_rows), side, 0)
    b_rows = ring_gather(rows_in[:, cut:], side, 0)
    b_rows = ring_gather(jnp.stack(b_rows), side, 1)
    group_rows = side * capacity

    def half_dot(rows, weight):
        return jnp.dot(rows.reshape(group_rows, cut), weight, preferred_element_type=jnp.float32)

    def both_halves(weight):
        from_a = jnp.stack([half_dot(r, weight[:cut]) for r in a_rows])
        from_b = jnp.stack([half_dot(r, weight[cut:]) for r in b_rows])
        ff = weight.shape[1]
        return from_a.reshape(side, side, capacity, ff) + from_b.reshape(
            side, side, capacity, ff
        ).transpose(1, 0, 2, 3)

    gate_part = both_halves(w_gate[0])
    up_part = both_halves(w_up[0])
    hidden_units = (jax.nn.silu(gate_part) * up_part).astype(jnp.bfloat16)
    ff_local = hidden_units.shape[-1]

    def down_group(units, weight):
        return (
            jnp.dot(units.reshape(group_rows, ff_local), weight, preferred_element_type=jnp.float32)
            .astype(jnp.bfloat16)
            .reshape(side, capacity, cut)
        )

    down_a = [down_group(hidden_units[k], w_down[0, :, :cut]) for k in range(side)]
    down_b = [down_group(hidden_units[:, k], w_down[0, :, cut:]) for k in range(side)]
    part_a = ring_scatter(down_a, side, 0).astype(jnp.bfloat16)
    part_a = ring_scatter([part_a[k] for k in range(side)], side, 1)
    part_b = ring_scatter(down_b, side, 1).astype(jnp.bfloat16)
    part_b = ring_scatter([part_b[k] for k in range(side)], side, 0)
    returned = jnp.concatenate([part_a, part_b], axis=1).astype(jnp.bfloat16)
    outbound = returned.reshape(capacity, exp_count, model_width // exp_count).transpose(1, 0, 2)
    homed = lax.all_to_all(outbound, "exp", split_axis=0, concat_axis=0, tiled=True)
    lookup = homed.reshape(NEXP * capacity, -1)
    chosen = (
        lookup[slot_grid.reshape(assign_count)]
        .astype(jnp.float32)
        .reshape(tok_rows, top_count, -1)
    )
    gate_share = gate_probs / jnp.sum(gate_probs, axis=1, keepdims=True)
    layer_out = (
        residual.astype(jnp.float32) + jnp.sum(gate_share[:, :, None] * chosen, axis=1)
    ).astype(jnp.bfloat16)
    return (layer_out, cache_pages)


def solution(mesh):
    return jax.shard_map(
        per_device,
        mesh=mesh,
        in_specs=(
            P("seq", "exp"),
            P("seq", "exp"),
            P("seq", "exp"),
            P("seq", "exp"),
            P(),
            P(),
            P("exp", None),
            P(),
            P("seq", None),
            P("seq", None),
            P("exp", None, "seq"),
            P("exp", None, "seq"),
            P("exp", "seq", None),
        ),
        out_specs=(P("seq", "exp"), P("seq", None, None, "exp")),
        check_vma=False,
    )
```

```python
import math

import jax
import jax.numpy as jnp
from jax import lax
from jax.sharding import PartitionSpec as P

HEAD_SIZE = 128
NEXP = 8
PAGE_TOKENS = 16


THETA = 1000000.0
EPS = 1e-05


def apply_rotary(values_in, positions, head_count):
    row_count = values_in.shape[0]
    split_view = values_in.astype(jnp.float32).reshape(row_count, head_count, HEAD_SIZE)
    steps_half = jnp.arange(HEAD_SIZE // 2, dtype=jnp.float32)
    frequency = THETA ** (-(2.0 * steps_half) / HEAD_SIZE)
    angles = positions.astype(jnp.float32)[:, None] * frequency[None, :]
    cosine = jnp.cos(angles)[:, None, :]
    sine_part = jnp.sin(angles)[:, None, :]
    front_half = split_view[..., : HEAD_SIZE // 2]
    back_half = split_view[..., HEAD_SIZE // 2 :]
    turned = jnp.concatenate(
        [front_half * cosine - back_half * sine_part, back_half * cosine + front_half * sine_part],
        axis=-1,
    )
    return turned.reshape(row_count, head_count * HEAD_SIZE).astype(jnp.bfloat16)


def shift_pairs(side, along, step):
    pairs = []
    for src in range(side * side):
        a, b = divmod(src, side)
        if along == 0:
            dst = ((a + step) % side) * side + b
        else:
            dst = a * side + (b + step) % side
        pairs.append((src, dst))
    return pairs


def ring_gather_whole(piece, perm_of):
    from_minus = lax.ppermute(piece, "seq", perm_of(1))
    from_plus = lax.ppermute(piece, "seq", perm_of(-1))
    far = lax.ppermute(from_minus, "seq", perm_of(1))
    return [piece, from_plus, far, from_minus]


def exp_ring_pairs(zside, step):
    pairs = []
    for src in range(zside * 2):
        z, core = divmod(src, 2)
        pairs.append((src, ((z + step) % zside) * 2 + core))
    return pairs


def scatter_exp(partial, exp_count):
    rows, width = partial.shape
    zside = exp_count // 2
    block = width // exp_count
    exp_index = lax.axis_index("exp")
    my_z, my_core = exp_index // 2, exp_index % 2
    grid = partial.astype(jnp.bfloat16).reshape(rows, zside, 2, block)
    mine = lax.dynamic_index_in_dim(grid, my_core, axis=2, keepdims=False)
    theirs = lax.dynamic_index_in_dim(grid, 1 - my_core, axis=2, keepdims=False)
    swapped = lax.ppermute(theirs, "exp", [(e, e ^ 1) for e in range(exp_count)])
    chip_sum = (mine.astype(jnp.float32) + swapped.astype(jnp.float32)).astype(jnp.bfloat16)
    parts = [
        lax.dynamic_index_in_dim(chip_sum, (my_z + k) % zside, axis=1, keepdims=False)
        for k in range(zside)
    ]
    cut = rows // 2
    far = parts[2]
    got_m = lax.ppermute(far[:cut], "exp", exp_ring_pairs(zside, 1))
    got_p = lax.ppermute(far[cut:], "exp", exp_ring_pairs(zside, -1))
    near_p = parts[1].astype(jnp.float32)
    near_p = jnp.concatenate([near_p[:cut] + got_m.astype(jnp.float32), near_p[cut:]], axis=0)
    near_m = parts[3].astype(jnp.float32)
    near_m = jnp.concatenate([near_m[:cut], near_m[cut:] + got_p.astype(jnp.float32)], axis=0)
    recv_m = lax.ppermute(near_p.astype(jnp.bfloat16), "exp", exp_ring_pairs(zside, 1))
    recv_p = lax.ppermute(near_m.astype(jnp.bfloat16), "exp", exp_ring_pairs(zside, -1))
    return parts[0].astype(jnp.float32) + recv_m.astype(jnp.float32) + recv_p.astype(jnp.float32)


def ring_gather(piece, side, along):
    from_minus = lax.ppermute(piece, "seq", shift_pairs(side, along, 1))
    from_plus = lax.ppermute(piece, "seq", shift_pairs(side, along, -1))
    cut = piece.shape[-2] // 2
    far_a = lax.ppermute(from_minus[..., :cut, :], "seq", shift_pairs(side, along, 1))
    far_b = lax.ppermute(from_plus[..., cut:, :], "seq", shift_pairs(side, along, -1))
    far = jnp.concatenate([far_a, far_b], axis=-2)
    return [piece, from_plus, far, from_minus]


def gather_2d(piece_a, piece_b, side):
    a_rows = ring_gather(piece_a, side, 1)
    a_rows = ring_gather(jnp.stack(a_rows), side, 0)
    b_rows = ring_gather(piece_b, side, 0)
    b_rows = ring_gather(jnp.stack(b_rows), side, 1)
    return jnp.stack(a_rows), jnp.stack(b_rows, axis=1)


def ring_scatter(parts, side, along):
    cut = parts[0].shape[-2] // 2
    far = parts[2]
    got_m = lax.ppermute(far[..., :cut, :], "seq", shift_pairs(side, along, 1))
    got_p = lax.ppermute(far[..., cut:, :], "seq", shift_pairs(side, along, -1))
    near_p = parts[1].astype(jnp.float32)
    near_p = jnp.concatenate(
        [near_p[..., :cut, :] + got_m.astype(jnp.float32), near_p[..., cut:, :]], axis=-2
    )
    near_m = parts[3].astype(jnp.float32)
    near_m = jnp.concatenate(
        [near_m[..., :cut, :], near_m[..., cut:, :] + got_p.astype(jnp.float32)], axis=-2
    )
    recv_m = lax.ppermute(near_p.astype(jnp.bfloat16), "seq", shift_pairs(side, along, 1))
    recv_p = lax.ppermute(near_m.astype(jnp.bfloat16), "seq", shift_pairs(side, along, -1))
    return parts[0].astype(jnp.float32) + recv_m.astype(jnp.float32) + recv_p.astype(jnp.float32)


def ring_scatter_whole(parts, side, along):
    got_m = lax.ppermute(parts[2], "seq", shift_pairs(side, along, 1))
    near_p = parts[1].astype(jnp.float32) + got_m.astype(jnp.float32)
    recv_m = lax.ppermute(near_p.astype(jnp.bfloat16), "seq", shift_pairs(side, along, 1))
    recv_p = lax.ppermute(parts[3], "seq", shift_pairs(side, along, -1))
    return parts[0].astype(jnp.float32) + recv_m.astype(jnp.float32) + recv_p.astype(jnp.float32)


def scatter_2d(out_a, out_b, side):
    part_a = ring_scatter([out_a[k] for k in range(side)], side, 0).astype(jnp.bfloat16)
    part_a = ring_scatter([part_a[k] for k in range(side)], side, 1)
    part_b = ring_scatter([out_b[:, k] for k in range(side)], side, 1).astype(jnp.bfloat16)
    part_b = ring_scatter([part_b[k] for k in range(side)], side, 0)
    return part_a, part_b


def per_device(
    hidden,
    queries,
    keys,
    values,
    block_place,
    page_table,
    out_weight,
    norm_gain,
    gate_probs,
    routes,
    w_gate,
    w_up,
    w_down,
):
    seq_count = lax.axis_size("seq")
    exp_count = lax.axis_size("exp")
    seq_index = lax.axis_index("seq")
    tok_rows = queries.shape[0]
    half_rows = tok_rows // 2
    all_rows = tok_rows * seq_count
    long_len = 3 * all_rows // 4
    side = math.isqrt(seq_count)
    my_x, my_y = seq_index // side, seq_index % side
    block_count = block_place.shape[0]
    all_pos = (
        block_place[:, None] * half_rows + jnp.arange(half_rows, dtype=jnp.int32)[None, :]
    ).reshape(all_rows)
    my_pos = lax.dynamic_slice_in_dim(all_pos, seq_index * tok_rows, tok_rows)
    my_long = my_pos >= long_len
    my_rope = my_pos - long_len * my_long.astype(jnp.int32)
    q_heads = queries.shape[1] // HEAD_SIZE
    kv_heads = keys.shape[1] // HEAD_SIZE
    query_head_group = q_heads // kv_heads
    query_rotated = apply_rotary(queries, my_rope, q_heads)
    key_rotated = apply_rotary(keys, my_rope, kv_heads)
    q_grid = query_rotated.reshape(tok_rows, kv_heads, query_head_group, HEAD_SIZE)
    score_scale = 1.0 / math.sqrt(HEAD_SIZE)
    page_count = tok_rows // PAGE_TOKENS
    page_total = page_table.shape[0]
    my_pages = seq_index * page_count + jnp.arange(page_count, dtype=jnp.int32)
    my_logical = jnp.sum(
        jnp.where(
            page_table[None, :] == my_pages[:, None],
            jnp.arange(page_total, dtype=jnp.int32)[None, :],
            0,
        ),
        axis=1,
    )
    slot_of_block = jnp.sum(
        jnp.where(
            block_place[None, :] == jnp.arange(block_count, dtype=jnp.int32)[:, None],
            jnp.arange(block_count, dtype=jnp.int32)[None, :],
            0,
        ),
        axis=1,
    )
    wanted_pos = (
        my_logical[:, None] * PAGE_TOKENS + jnp.arange(PAGE_TOKENS, dtype=jnp.int32)[None, :]
    ).reshape(page_count * PAGE_TOKENS)
    taken_abs = slot_of_block[wanted_pos // half_rows] * half_rows + wanted_pos % half_rows
    taken = taken_abs
    kv_width = key_rotated.shape[1]
    kv_piece = jnp.concatenate([key_rotated, values], axis=1)
    kv_all = lax.all_to_all(
        jnp.broadcast_to(kv_piece[None], (seq_count,) + kv_piece.shape),
        "seq",
        split_axis=0,
        concat_axis=0,
        tiled=True,
    ).reshape(all_rows, 2 * kv_width)
    key_all, value_all = kv_all[:, :kv_width], kv_all[:, kv_width:]
    peak_old = jnp.full((kv_heads, query_head_group, tok_rows), -1e30, jnp.float32)
    row_count = key_all.shape[0]
    scores = (
        jnp.einsum(
            "tkgd,nkd->kgtn",
            q_grid,
            key_all.reshape(row_count, kv_heads, HEAD_SIZE),
            preferred_element_type=jnp.float32,
        )
        * score_scale
    )
    allowed = ((all_pos >= long_len)[None, :] == my_long[:, None]) & (
        all_pos[None, :] <= my_pos[:, None]
    )
    scores = jnp.where(allowed, scores, -1e30)
    peak_new = jnp.maximum(peak_old, jnp.max(scores, axis=-1))
    weights = jnp.where(allowed, jnp.exp(scores - peak_new[..., None]), 0.0)
    total_new = jnp.sum(weights, axis=-1)
    summed = jnp.einsum(
        "kgtn,nkd->kgtd",
        weights.astype(jnp.bfloat16),
        value_all.reshape(row_count, kv_heads, HEAD_SIZE),
        preferred_element_type=jnp.float32,
    )
    peak_final, total_final, summed = (peak_new, total_new, summed)
    cache_pages = jnp.stack([key_all[taken], value_all[taken]], axis=1).reshape(
        page_count, PAGE_TOKENS, 2, kv_heads * HEAD_SIZE
    )
    attended = (
        (summed / total_final[..., None])
        .transpose(2, 0, 1, 3)
        .reshape(tok_rows, q_heads * HEAD_SIZE)
        .astype(jnp.bfloat16)
    )
    partial_proj = jnp.dot(attended, out_weight, preferred_element_type=jnp.float32)
    proj_width = partial_proj.shape[1] // exp_count
    proj_blocks = lax.all_to_all(
        partial_proj.astype(jnp.bfloat16).reshape(tok_rows, exp_count, proj_width).transpose(1, 0, 2),
        "exp",
        split_axis=0,
        concat_axis=0,
        tiled=True,
    )
    projected = jnp.sum(proj_blocks.astype(jnp.float32), axis=0)
    residual = (hidden.astype(jnp.float32) + projected).astype(jnp.bfloat16)
    top_count = routes.shape[1]
    capacity = tok_rows // 2
    assign_count = tok_rows * top_count
    flat_routes = routes.reshape(assign_count)
    expert_hot = (flat_routes[:, None] == jnp.arange(NEXP, dtype=jnp.int32)[None, :]).astype(
        jnp.float32
    )
    earlier = (jnp.arange(assign_count)[:, None] > jnp.arange(assign_count)[None, :]).astype(
        jnp.float32
    )
    before = jnp.dot(earlier, expert_hot, preferred_element_type=jnp.float32)
    slot_rank = jnp.sum(before * expert_hot, axis=1).astype(jnp.int32).reshape(tok_rows, top_count)
    slot_grid = routes * capacity + slot_rank
    chooser = jnp.any(
        slot_grid[None, :, :] == jnp.arange(NEXP * capacity, dtype=jnp.int32)[:, None, None],
        axis=-1,
    ).astype(jnp.bfloat16)
    outgoing_rows = jnp.dot(chooser, residual, preferred_element_type=jnp.float32).astype(
        jnp.bfloat16
    )
    expert_local = NEXP // exp_count
    arrived_rows = lax.all_to_all(
        outgoing_rows.reshape(exp_count, expert_local * capacity, -1),
        "exp",
        split_axis=0,
        concat_axis=2,
        tiled=True,
    )
    gathered_in = arrived_rows.astype(jnp.float32)
    mean_square = jnp.mean(gathered_in * gathered_in, axis=-1, keepdims=True)
    normed = (gathered_in * lax.rsqrt(mean_square + EPS) * norm_gain).astype(jnp.bfloat16)
    rows_in = normed[0]
    model_width = rows_in.shape[1]
    cut = model_width // 2
    a_rows = ring_gather(rows_in[:, :cut], side, 1)
    a_rows = ring_gather(jnp.stack(a_rows), side, 0)
    b_rows = ring_gather(rows_in[:, cut:], side, 0)
    b_rows = ring_gather(jnp.stack(b_rows), side, 1)
    group_rows = side * capacity

    def half_dot(rows, weight):
        return jnp.dot(rows.reshape(group_rows, cut), weight, preferred_element_type=jnp.float32)

    def both_halves(weight):
        from_a = jnp.stack([half_dot(r, weight[:cut]) for r in a_rows])
        from_b = jnp.stack([half_dot(r, weight[cut:]) for r in b_rows])
        ff = weight.shape[1]
        return from_a.reshape(side, side, capacity, ff) + from_b.reshape(
            side, side, capacity, ff
        ).transpose(1, 0, 2, 3)

    gate_part = both_halves(w_gate[0])
    up_part = both_halves(w_up[0])
    hidden_units = (jax.nn.silu(gate_part) * up_part).astype(jnp.bfloat16)
    ff_local = hidden_units.shape[-1]

    def down_group(units, weight):
        return (
            jnp.dot(units.reshape(group_rows, ff_local), weight, preferred_element_type=jnp.float32)
            .astype(jnp.bfloat16)
            .reshape(side, capacity, cut)
        )

    down_a = [down_group(hidden_units[k], w_down[0, :, :cut]) for k in range(side)]
    down_b = [down_group(hidden_units[:, k], w_down[0, :, cut:]) for k in range(side)]
    part_a = ring_scatter(down_a, side, 0).astype(jnp.bfloat16)
    part_a = ring_scatter_whole([part_a[k] for k in range(side)], side, 1)
    part_b = ring_scatter(down_b, side, 1).astype(jnp.bfloat16)
    part_b = ring_scatter_whole([part_b[k] for k in range(side)], side, 0)
    returned = jnp.concatenate([part_a, part_b], axis=1).astype(jnp.bfloat16)
    outbound = returned.reshape(capacity, exp_count, model_width // exp_count).transpose(1, 0, 2)
    homed = lax.all_to_all(outbound, "exp", split_axis=0, concat_axis=0, tiled=True)
    lookup = homed.reshape(NEXP * capacity, -1)
    chosen = (
        lookup[slot_grid.reshape(assign_count)]
        .astype(jnp.float32)
        .reshape(tok_rows, top_count, -1)
    )
    gate_share = gate_probs / jnp.sum(gate_probs, axis=1, keepdims=True)
    layer_out = (
        residual.astype(jnp.float32) + jnp.sum(gate_share[:, :, None] * chosen, axis=1)
    ).astype(jnp.bfloat16)
    return (layer_out, cache_pages)


def solution(mesh):
    return jax.shard_map(
        per_device,
        mesh=mesh,
        in_specs=(
            P("seq", "exp"),
            P("seq", "exp"),
            P("seq", "exp"),
            P("seq", "exp"),
            P(),
            P(),
            P("exp", None),
            P(),
            P("seq", None),
            P("seq", None),
            P("exp", None, "seq"),
            P("exp", None, "seq"),
            P("exp", "seq", None),
        ),
        out_specs=(P("seq", "exp"), P("seq", None, None, "exp")),
        check_vma=False,
    )
```

```python
import math

import jax
import jax.numpy as jnp
from jax import lax
from jax.sharding import PartitionSpec as P

HEAD_SIZE = 128
NEXP = 8
PAGE_TOKENS = 16


THETA = 1000000.0
EPS = 1e-05


def apply_rotary(values_in, positions, head_count):
    row_count = values_in.shape[0]
    split_view = values_in.astype(jnp.float32).reshape(row_count, head_count, HEAD_SIZE)
    steps_half = jnp.arange(HEAD_SIZE // 2, dtype=jnp.float32)
    frequency = THETA ** (-(2.0 * steps_half) / HEAD_SIZE)
    angles = positions.astype(jnp.float32)[:, None] * frequency[None, :]
    cosine = jnp.cos(angles)[:, None, :]
    sine_part = jnp.sin(angles)[:, None, :]
    front_half = split_view[..., : HEAD_SIZE // 2]
    back_half = split_view[..., HEAD_SIZE // 2 :]
    turned = jnp.concatenate(
        [front_half * cosine - back_half * sine_part, back_half * cosine + front_half * sine_part],
        axis=-1,
    )
    return turned.reshape(row_count, head_count * HEAD_SIZE).astype(jnp.bfloat16)


def shift_pairs(side, along, step):
    pairs = []
    for src in range(side * side):
        a, b = divmod(src, side)
        if along == 0:
            dst = ((a + step) % side) * side + b
        else:
            dst = a * side + (b + step) % side
        pairs.append((src, dst))
    return pairs


def ring_gather_whole(piece, perm_of):
    from_minus = lax.ppermute(piece, "seq", perm_of(1))
    from_plus = lax.ppermute(piece, "seq", perm_of(-1))
    far = lax.ppermute(from_minus, "seq", perm_of(1))
    return [piece, from_plus, far, from_minus]


def exp_ring_pairs(zside, step):
    pairs = []
    for src in range(zside * 2):
        z, core = divmod(src, 2)
        pairs.append((src, ((z + step) % zside) * 2 + core))
    return pairs


def scatter_exp(partial, exp_count):
    rows, width = partial.shape
    zside = exp_count // 2
    block = width // exp_count
    exp_index = lax.axis_index("exp")
    my_z, my_core = exp_index // 2, exp_index % 2
    grid = partial.astype(jnp.bfloat16).reshape(rows, zside, 2, block)
    mine = lax.dynamic_index_in_dim(grid, my_core, axis=2, keepdims=False)
    theirs = lax.dynamic_index_in_dim(grid, 1 - my_core, axis=2, keepdims=False)
    swapped = lax.ppermute(theirs, "exp", [(e, e ^ 1) for e in range(exp_count)])
    chip_sum = (mine.astype(jnp.float32) + swapped.astype(jnp.float32)).astype(jnp.bfloat16)
    parts = [
        lax.dynamic_index_in_dim(chip_sum, (my_z + k) % zside, axis=1, keepdims=False)
        for k in range(zside)
    ]
    cut = rows // 2
    far = parts[2]
    got_m = lax.ppermute(far[:cut], "exp", exp_ring_pairs(zside, 1))
    got_p = lax.ppermute(far[cut:], "exp", exp_ring_pairs(zside, -1))
    near_p = parts[1].astype(jnp.float32)
    near_p = jnp.concatenate([near_p[:cut] + got_m.astype(jnp.float32), near_p[cut:]], axis=0)
    near_m = parts[3].astype(jnp.float32)
    near_m = jnp.concatenate([near_m[:cut], near_m[cut:] + got_p.astype(jnp.float32)], axis=0)
    recv_m = lax.ppermute(near_p.astype(jnp.bfloat16), "exp", exp_ring_pairs(zside, 1))
    recv_p = lax.ppermute(near_m.astype(jnp.bfloat16), "exp", exp_ring_pairs(zside, -1))
    return parts[0].astype(jnp.float32) + recv_m.astype(jnp.float32) + recv_p.astype(jnp.float32)


def ring_gather(piece, side, along):
    from_minus = lax.ppermute(piece, "seq", shift_pairs(side, along, 1))
    from_plus = lax.ppermute(piece, "seq", shift_pairs(side, along, -1))
    cut = piece.shape[-2] // 2
    far_a = lax.ppermute(from_minus[..., :cut, :], "seq", shift_pairs(side, along, 1))
    far_b = lax.ppermute(from_plus[..., cut:, :], "seq", shift_pairs(side, along, -1))
    far = jnp.concatenate([far_a, far_b], axis=-2)
    return [piece, from_plus, far, from_minus]


def gather_2d(piece_a, piece_b, side):
    a_rows = ring_gather(piece_a, side, 1)
    a_rows = ring_gather(jnp.stack(a_rows), side, 0)
    b_rows = ring_gather(piece_b, side, 0)
    b_rows = ring_gather(jnp.stack(b_rows), side, 1)
    return jnp.stack(a_rows), jnp.stack(b_rows, axis=1)


def ring_scatter(parts, side, along):
    cut = parts[0].shape[-2] // 2
    far = parts[2]
    got_m = lax.ppermute(far[..., :cut, :], "seq", shift_pairs(side, along, 1))
    got_p = lax.ppermute(far[..., cut:, :], "seq", shift_pairs(side, along, -1))
    near_p = parts[1].astype(jnp.float32)
    near_p = jnp.concatenate(
        [near_p[..., :cut, :] + got_m.astype(jnp.float32), near_p[..., cut:, :]], axis=-2
    )
    near_m = parts[3].astype(jnp.float32)
    near_m = jnp.concatenate(
        [near_m[..., :cut, :], near_m[..., cut:, :] + got_p.astype(jnp.float32)], axis=-2
    )
    recv_m = lax.ppermute(near_p.astype(jnp.bfloat16), "seq", shift_pairs(side, along, 1))
    recv_p = lax.ppermute(near_m.astype(jnp.bfloat16), "seq", shift_pairs(side, along, -1))
    return parts[0].astype(jnp.float32) + recv_m.astype(jnp.float32) + recv_p.astype(jnp.float32)


def scatter_2d(out_a, out_b, side):
    part_a = ring_scatter([out_a[k] for k in range(side)], side, 0).astype(jnp.bfloat16)
    part_a = ring_scatter([part_a[k] for k in range(side)], side, 1)
    part_b = ring_scatter([out_b[:, k] for k in range(side)], side, 1).astype(jnp.bfloat16)
    part_b = ring_scatter([part_b[k] for k in range(side)], side, 0)
    return part_a, part_b


def per_device(
    hidden,
    queries,
    keys,
    values,
    block_place,
    page_table,
    out_weight,
    norm_gain,
    gate_probs,
    routes,
    w_gate,
    w_up,
    w_down,
):
    seq_count = lax.axis_size("seq")
    exp_count = lax.axis_size("exp")
    seq_index = lax.axis_index("seq")
    tok_rows = queries.shape[0]
    half_rows = tok_rows // 2
    all_rows = tok_rows * seq_count
    long_len = 3 * all_rows // 4
    side = math.isqrt(seq_count)
    my_x, my_y = seq_index // side, seq_index % side
    block_count = block_place.shape[0]
    all_pos = (
        block_place[:, None] * half_rows + jnp.arange(half_rows, dtype=jnp.int32)[None, :]
    ).reshape(all_rows)
    my_pos = lax.dynamic_slice_in_dim(all_pos, seq_index * tok_rows, tok_rows)
    my_long = my_pos >= long_len
    my_rope = my_pos - long_len * my_long.astype(jnp.int32)
    q_heads = queries.shape[1] // HEAD_SIZE
    kv_heads = keys.shape[1] // HEAD_SIZE
    query_head_group = q_heads // kv_heads
    query_rotated = apply_rotary(queries, my_rope, q_heads)
    key_rotated = apply_rotary(keys, my_rope, kv_heads)
    q_grid = query_rotated.reshape(tok_rows, kv_heads, query_head_group, HEAD_SIZE)
    score_scale = 1.0 / math.sqrt(HEAD_SIZE)
    page_count = tok_rows // PAGE_TOKENS
    page_total = page_table.shape[0]
    my_pages = seq_index * page_count + jnp.arange(page_count, dtype=jnp.int32)
    my_logical = jnp.sum(
        jnp.where(
            page_table[None, :] == my_pages[:, None],
            jnp.arange(page_total, dtype=jnp.int32)[None, :],
            0,
        ),
        axis=1,
    )
    slot_of_block = jnp.sum(
        jnp.where(
            block_place[None, :] == jnp.arange(block_count, dtype=jnp.int32)[:, None],
            jnp.arange(block_count, dtype=jnp.int32)[None, :],
            0,
        ),
        axis=1,
    )
    wanted_pos = (
        my_logical[:, None] * PAGE_TOKENS + jnp.arange(PAGE_TOKENS, dtype=jnp.int32)[None, :]
    ).reshape(page_count * PAGE_TOKENS)
    taken_abs = slot_of_block[wanted_pos // half_rows] * half_rows + wanted_pos % half_rows
    taken = taken_abs
    kv_width = key_rotated.shape[1]
    kv_piece = jnp.concatenate([key_rotated, values], axis=1)
    kv_all = lax.all_to_all(
        jnp.broadcast_to(kv_piece[None], (seq_count,) + kv_piece.shape),
        "seq",
        split_axis=0,
        concat_axis=0,
        tiled=True,
    ).reshape(all_rows, 2 * kv_width)
    key_all, value_all = kv_all[:, :kv_width], kv_all[:, kv_width:]
    peak_old = jnp.full((kv_heads, query_head_group, tok_rows), -1e30, jnp.float32)
    row_count = key_all.shape[0]
    scores = (
        jnp.einsum(
            "tkgd,nkd->kgtn",
            q_grid,
            key_all.reshape(row_count, kv_heads, HEAD_SIZE),
            preferred_element_type=jnp.float32,
        )
        * score_scale
    )
    allowed = ((all_pos >= long_len)[None, :] == my_long[:, None]) & (
        all_pos[None, :] <= my_pos[:, None]
    )
    scores = jnp.where(allowed, scores, -1e30)
    peak_new = jnp.maximum(peak_old, jnp.max(scores, axis=-1))
    weights = jnp.where(allowed, jnp.exp(scores - peak_new[..., None]), 0.0)
    total_new = jnp.sum(weights, axis=-1)
    summed = jnp.einsum(
        "kgtn,nkd->kgtd",
        weights.astype(jnp.bfloat16),
        value_all.reshape(row_count, kv_heads, HEAD_SIZE),
        preferred_element_type=jnp.float32,
    )
    peak_final, total_final, summed = (peak_new, total_new, summed)
    cache_pages = jnp.stack([key_all[taken], value_all[taken]], axis=1).reshape(
        page_count, PAGE_TOKENS, 2, kv_heads * HEAD_SIZE
    )
    attended = (
        (summed / total_final[..., None])
        .transpose(2, 0, 1, 3)
        .reshape(tok_rows, q_heads * HEAD_SIZE)
        .astype(jnp.bfloat16)
    )
    partial_proj = jnp.dot(attended, out_weight, preferred_element_type=jnp.float32)
    projected = scatter_exp(partial_proj, exp_count)
    residual = (hidden.astype(jnp.float32) + projected).astype(jnp.bfloat16)
    top_count = routes.shape[1]
    capacity = tok_rows // 2
    assign_count = tok_rows * top_count
    flat_routes = routes.reshape(assign_count)
    expert_hot = (flat_routes[:, None] == jnp.arange(NEXP, dtype=jnp.int32)[None, :]).astype(
        jnp.float32
    )
    earlier = (jnp.arange(assign_count)[:, None] > jnp.arange(assign_count)[None, :]).astype(
        jnp.float32
    )
    before = jnp.dot(earlier, expert_hot, preferred_element_type=jnp.float32)
    slot_rank = jnp.sum(before * expert_hot, axis=1).astype(jnp.int32).reshape(tok_rows, top_count)
    slot_grid = routes * capacity + slot_rank
    chooser = jnp.any(
        slot_grid[None, :, :] == jnp.arange(NEXP * capacity, dtype=jnp.int32)[:, None, None],
        axis=-1,
    ).astype(jnp.bfloat16)
    outgoing_rows = jnp.dot(chooser, residual, preferred_element_type=jnp.float32).astype(
        jnp.bfloat16
    )
    expert_local = NEXP // exp_count
    arrived_rows = lax.all_to_all(
        outgoing_rows.reshape(exp_count, expert_local * capacity, -1),
        "exp",
        split_axis=0,
        concat_axis=2,
        tiled=True,
    )
    gathered_in = arrived_rows.astype(jnp.float32)
    mean_square = jnp.mean(gathered_in * gathered_in, axis=-1, keepdims=True)
    normed = (gathered_in * lax.rsqrt(mean_square + EPS) * norm_gain).astype(jnp.bfloat16)
    rows_in = normed[0]
    model_width = rows_in.shape[1]
    cut = model_width // 2
    a_rows = ring_gather(rows_in[:, :cut], side, 1)
    a_rows = ring_gather(jnp.stack(a_rows), side, 0)
    b_rows = ring_gather(rows_in[:, cut:], side, 0)
    b_rows = ring_gather(jnp.stack(b_rows), side, 1)
    group_rows = side * capacity

    def half_dot(rows, weight):
        return jnp.dot(rows.reshape(group_rows, cut), weight, preferred_element_type=jnp.float32)

    def both_halves(weight):
        from_a = jnp.stack([half_dot(r, weight[:cut]) for r in a_rows])
        from_b = jnp.stack([half_dot(r, weight[cut:]) for r in b_rows])
        ff = weight.shape[1]
        return from_a.reshape(side, side, capacity, ff) + from_b.reshape(
            side, side, capacity, ff
        ).transpose(1, 0, 2, 3)

    gate_part = both_halves(w_gate[0])
    up_part = both_halves(w_up[0])
    hidden_units = (jax.nn.silu(gate_part) * up_part).astype(jnp.bfloat16)
    ff_local = hidden_units.shape[-1]

    def down_group(units, weight):
        return (
            jnp.dot(units.reshape(group_rows, ff_local), weight, preferred_element_type=jnp.float32)
            .astype(jnp.bfloat16)
            .reshape(side, capacity, cut)
        )

    far_group = side // 2
    far_a = down_group(hidden_units[far_group], w_down[0, :, :cut])
    far_b = down_group(hidden_units[:, far_group], w_down[0, :, cut:])
    far_a, far_b, units_rest = lax.optimization_barrier((far_a, far_b, hidden_units))
    down_a = [
        far_a if k == far_group else down_group(units_rest[k], w_down[0, :, :cut])
        for k in range(side)
    ]
    down_b = [
        far_b if k == far_group else down_group(units_rest[:, k], w_down[0, :, cut:])
        for k in range(side)
    ]
    part_a = ring_scatter(down_a, side, 0).astype(jnp.bfloat16)
    part_a = ring_scatter([part_a[k] for k in range(side)], side, 1)
    part_b = ring_scatter(down_b, side, 1).astype(jnp.bfloat16)
    part_b = ring_scatter([part_b[k] for k in range(side)], side, 0)
    returned = jnp.concatenate([part_a, part_b], axis=1).astype(jnp.bfloat16)
    outbound = returned.reshape(capacity, exp_count, model_width // exp_count).transpose(1, 0, 2)
    homed = lax.all_to_all(outbound, "exp", split_axis=0, concat_axis=0, tiled=True)
    lookup = homed.reshape(NEXP * capacity, -1)
    chosen = (
        lookup[slot_grid.reshape(assign_count)]
        .astype(jnp.float32)
        .reshape(tok_rows, top_count, -1)
    )
    gate_share = gate_probs / jnp.sum(gate_probs, axis=1, keepdims=True)
    layer_out = (
        residual.astype(jnp.float32) + jnp.sum(gate_share[:, :, None] * chosen, axis=1)
    ).astype(jnp.bfloat16)
    return (layer_out, cache_pages)


def solution(mesh):
    return jax.shard_map(
        per_device,
        mesh=mesh,
        in_specs=(
            P("seq", "exp"),
            P("seq", "exp"),
            P("seq", "exp"),
            P("seq", "exp"),
            P(),
            P(),
            P("exp", None),
            P(),
            P("seq", None),
            P("seq", None),
            P("exp", None, "seq"),
            P("exp", None, "seq"),
            P("exp", "seq", None),
        ),
        out_specs=(P("seq", "exp"), P("seq", None, None, "exp")),
        check_vma=False,
    )
```

```python
import math

import jax
import jax.numpy as jnp
from jax import lax
from jax.sharding import PartitionSpec as P

HEAD_SIZE = 128
NEXP = 8
PAGE_TOKENS = 16


THETA = 1000000.0
EPS = 1e-05


def apply_rotary(values_in, positions, head_count):
    row_count = values_in.shape[0]
    split_view = values_in.astype(jnp.float32).reshape(row_count, head_count, HEAD_SIZE)
    steps_half = jnp.arange(HEAD_SIZE // 2, dtype=jnp.float32)
    frequency = THETA ** (-(2.0 * steps_half) / HEAD_SIZE)
    angles = positions.astype(jnp.float32)[:, None] * frequency[None, :]
    cosine = jnp.cos(angles)[:, None, :]
    sine_part = jnp.sin(angles)[:, None, :]
    front_half = split_view[..., : HEAD_SIZE // 2]
    back_half = split_view[..., HEAD_SIZE // 2 :]
    turned = jnp.concatenate(
        [front_half * cosine - back_half * sine_part, back_half * cosine + front_half * sine_part],
        axis=-1,
    )
    return turned.reshape(row_count, head_count * HEAD_SIZE).astype(jnp.bfloat16)


def shift_pairs(side, along, step):
    pairs = []
    for src in range(side * side):
        a, b = divmod(src, side)
        if along == 0:
            dst = ((a + step) % side) * side + b
        else:
            dst = a * side + (b + step) % side
        pairs.append((src, dst))
    return pairs


def ring_gather_whole(piece, perm_of):
    from_minus = lax.ppermute(piece, "seq", perm_of(1))
    from_plus = lax.ppermute(piece, "seq", perm_of(-1))
    far = lax.ppermute(from_minus, "seq", perm_of(1))
    return [piece, from_plus, far, from_minus]


def exp_ring_pairs(zside, step):
    pairs = []
    for src in range(zside * 2):
        z, core = divmod(src, 2)
        pairs.append((src, ((z + step) % zside) * 2 + core))
    return pairs


def scatter_exp(partial, exp_count):
    rows, width = partial.shape
    zside = exp_count // 2
    block = width // exp_count
    exp_index = lax.axis_index("exp")
    my_z, my_core = exp_index // 2, exp_index % 2
    grid = partial.astype(jnp.bfloat16).reshape(rows, zside, 2, block)
    mine = lax.dynamic_index_in_dim(grid, my_core, axis=2, keepdims=False)
    theirs = lax.dynamic_index_in_dim(grid, 1 - my_core, axis=2, keepdims=False)
    swapped = lax.ppermute(theirs, "exp", [(e, e ^ 1) for e in range(exp_count)])
    chip_sum = (mine.astype(jnp.float32) + swapped.astype(jnp.float32)).astype(jnp.bfloat16)
    parts = [
        lax.dynamic_index_in_dim(chip_sum, (my_z + k) % zside, axis=1, keepdims=False)
        for k in range(zside)
    ]
    cut = rows // 2
    far = parts[2]
    got_m = lax.ppermute(far[:cut], "exp", exp_ring_pairs(zside, 1))
    got_p = lax.ppermute(far[cut:], "exp", exp_ring_pairs(zside, -1))
    near_p = parts[1].astype(jnp.float32)
    near_p = jnp.concatenate([near_p[:cut] + got_m.astype(jnp.float32), near_p[cut:]], axis=0)
    near_m = parts[3].astype(jnp.float32)
    near_m = jnp.concatenate([near_m[:cut], near_m[cut:] + got_p.astype(jnp.float32)], axis=0)
    recv_m = lax.ppermute(near_p.astype(jnp.bfloat16), "exp", exp_ring_pairs(zside, 1))
    recv_p = lax.ppermute(near_m.astype(jnp.bfloat16), "exp", exp_ring_pairs(zside, -1))
    return parts[0].astype(jnp.float32) + recv_m.astype(jnp.float32) + recv_p.astype(jnp.float32)


def ring_gather(piece, side, along):
    from_minus = lax.ppermute(piece, "seq", shift_pairs(side, along, 1))
    from_plus = lax.ppermute(piece, "seq", shift_pairs(side, along, -1))
    cut = piece.shape[-2] // 2
    far_a = lax.ppermute(from_minus[..., :cut, :], "seq", shift_pairs(side, along, 1))
    far_b = lax.ppermute(from_plus[..., cut:, :], "seq", shift_pairs(side, along, -1))
    far = jnp.concatenate([far_a, far_b], axis=-2)
    return [piece, from_plus, far, from_minus]


def gather_2d(piece_a, piece_b, side):
    a_rows = ring_gather(piece_a, side, 1)
    a_rows = ring_gather(jnp.stack(a_rows), side, 0)
    b_rows = ring_gather(piece_b, side, 0)
    b_rows = ring_gather(jnp.stack(b_rows), side, 1)
    return jnp.stack(a_rows), jnp.stack(b_rows, axis=1)


def ring_scatter(parts, side, along):
    cut = parts[0].shape[-2] // 2
    far = parts[2]
    got_m = lax.ppermute(far[..., :cut, :], "seq", shift_pairs(side, along, 1))
    got_p = lax.ppermute(far[..., cut:, :], "seq", shift_pairs(side, along, -1))
    near_p = parts[1].astype(jnp.float32)
    near_p = jnp.concatenate(
        [near_p[..., :cut, :] + got_m.astype(jnp.float32), near_p[..., cut:, :]], axis=-2
    )
    near_m = parts[3].astype(jnp.float32)
    near_m = jnp.concatenate(
        [near_m[..., :cut, :], near_m[..., cut:, :] + got_p.astype(jnp.float32)], axis=-2
    )
    recv_m = lax.ppermute(near_p.astype(jnp.bfloat16), "seq", shift_pairs(side, along, 1))
    recv_p = lax.ppermute(near_m.astype(jnp.bfloat16), "seq", shift_pairs(side, along, -1))
    return parts[0].astype(jnp.float32) + recv_m.astype(jnp.float32) + recv_p.astype(jnp.float32)


def ring_scatter_whole(parts, side, along):
    got_m = lax.ppermute(parts[2], "seq", shift_pairs(side, along, 1))
    near_p = parts[1].astype(jnp.float32) + got_m.astype(jnp.float32)
    recv_m = lax.ppermute(near_p.astype(jnp.bfloat16), "seq", shift_pairs(side, along, 1))
    recv_p = lax.ppermute(parts[3], "seq", shift_pairs(side, along, -1))
    return parts[0].astype(jnp.float32) + recv_m.astype(jnp.float32) + recv_p.astype(jnp.float32)


def scatter_2d(out_a, out_b, side):
    part_a = ring_scatter([out_a[k] for k in range(side)], side, 0).astype(jnp.bfloat16)
    part_a = ring_scatter([part_a[k] for k in range(side)], side, 1)
    part_b = ring_scatter([out_b[:, k] for k in range(side)], side, 1).astype(jnp.bfloat16)
    part_b = ring_scatter([part_b[k] for k in range(side)], side, 0)
    return part_a, part_b


def per_device(
    hidden,
    queries,
    keys,
    values,
    block_place,
    page_table,
    out_weight,
    norm_gain,
    gate_probs,
    routes,
    w_gate,
    w_up,
    w_down,
):
    seq_count = lax.axis_size("seq")
    exp_count = lax.axis_size("exp")
    seq_index = lax.axis_index("seq")
    tok_rows = queries.shape[0]
    half_rows = tok_rows // 2
    all_rows = tok_rows * seq_count
    long_len = 3 * all_rows // 4
    side = math.isqrt(seq_count)
    my_x, my_y = seq_index // side, seq_index % side
    block_count = block_place.shape[0]
    all_pos = (
        block_place[:, None] * half_rows + jnp.arange(half_rows, dtype=jnp.int32)[None, :]
    ).reshape(all_rows)
    my_pos = lax.dynamic_slice_in_dim(all_pos, seq_index * tok_rows, tok_rows)
    my_long = my_pos >= long_len
    my_rope = my_pos - long_len * my_long.astype(jnp.int32)
    q_heads = queries.shape[1] // HEAD_SIZE
    kv_heads = keys.shape[1] // HEAD_SIZE
    query_head_group = q_heads // kv_heads
    query_rotated = apply_rotary(queries, my_rope, q_heads)
    key_rotated = apply_rotary(keys, my_rope, kv_heads)
    q_grid = query_rotated.reshape(tok_rows, kv_heads, query_head_group, HEAD_SIZE)
    score_scale = 1.0 / math.sqrt(HEAD_SIZE)
    page_count = tok_rows // PAGE_TOKENS
    page_total = page_table.shape[0]
    my_pages = seq_index * page_count + jnp.arange(page_count, dtype=jnp.int32)
    my_logical = jnp.sum(
        jnp.where(
            page_table[None, :] == my_pages[:, None],
            jnp.arange(page_total, dtype=jnp.int32)[None, :],
            0,
        ),
        axis=1,
    )
    slot_of_block = jnp.sum(
        jnp.where(
            block_place[None, :] == jnp.arange(block_count, dtype=jnp.int32)[:, None],
            jnp.arange(block_count, dtype=jnp.int32)[None, :],
            0,
        ),
        axis=1,
    )
    wanted_pos = (
        my_logical[:, None] * PAGE_TOKENS + jnp.arange(PAGE_TOKENS, dtype=jnp.int32)[None, :]
    ).reshape(page_count * PAGE_TOKENS)
    taken_abs = slot_of_block[wanted_pos // half_rows] * half_rows + wanted_pos % half_rows
    taken = taken_abs
    kv_width = key_rotated.shape[1]
    kv_piece = jnp.concatenate([key_rotated, values], axis=1)
    kv_all = lax.all_to_all(
        jnp.broadcast_to(kv_piece[None], (seq_count,) + kv_piece.shape),
        "seq",
        split_axis=0,
        concat_axis=0,
        tiled=True,
    ).reshape(all_rows, 2 * kv_width)
    key_all, value_all = kv_all[:, :kv_width], kv_all[:, kv_width:]
    peak_old = jnp.full((kv_heads, query_head_group, tok_rows), -1e30, jnp.float32)
    row_count = key_all.shape[0]
    scores = (
        jnp.einsum(
            "tkgd,nkd->kgtn",
            q_grid,
            key_all.reshape(row_count, kv_heads, HEAD_SIZE),
            preferred_element_type=jnp.float32,
        )
        * score_scale
    )
    allowed = ((all_pos >= long_len)[None, :] == my_long[:, None]) & (
        all_pos[None, :] <= my_pos[:, None]
    )
    scores = jnp.where(allowed, scores, -1e30)
    peak_new = jnp.maximum(peak_old, jnp.max(scores, axis=-1))
    weights = jnp.where(allowed, jnp.exp(scores - peak_new[..., None]), 0.0)
    total_new = jnp.sum(weights, axis=-1)
    summed = jnp.einsum(
        "kgtn,nkd->kgtd",
        weights.astype(jnp.bfloat16),
        value_all.reshape(row_count, kv_heads, HEAD_SIZE),
        preferred_element_type=jnp.float32,
    )
    peak_final, total_final, summed = (peak_new, total_new, summed)
    cache_pages = jnp.stack([key_all[taken], value_all[taken]], axis=1).reshape(
        page_count, PAGE_TOKENS, 2, kv_heads * HEAD_SIZE
    )
    attended = (
        (summed / total_final[..., None])
        .transpose(2, 0, 1, 3)
        .reshape(tok_rows, q_heads * HEAD_SIZE)
        .astype(jnp.bfloat16)
    )
    partial_proj = jnp.dot(attended, out_weight, preferred_element_type=jnp.float32)
    projected = scatter_exp(partial_proj, exp_count)
    residual = (hidden.astype(jnp.float32) + projected).astype(jnp.bfloat16)
    top_count = routes.shape[1]
    capacity = tok_rows // 2
    assign_count = tok_rows * top_count
    flat_routes = routes.reshape(assign_count)
    expert_hot = (flat_routes[:, None] == jnp.arange(NEXP, dtype=jnp.int32)[None, :]).astype(
        jnp.float32
    )
    earlier = (jnp.arange(assign_count)[:, None] > jnp.arange(assign_count)[None, :]).astype(
        jnp.float32
    )
    before = jnp.dot(earlier, expert_hot, preferred_element_type=jnp.float32)
    slot_rank = jnp.sum(before * expert_hot, axis=1).astype(jnp.int32).reshape(tok_rows, top_count)
    slot_grid = routes * capacity + slot_rank
    chooser = jnp.any(
        slot_grid[None, :, :] == jnp.arange(NEXP * capacity, dtype=jnp.int32)[:, None, None],
        axis=-1,
    ).astype(jnp.bfloat16)
    outgoing_rows = jnp.dot(chooser, residual, preferred_element_type=jnp.float32).astype(
        jnp.bfloat16
    )
    expert_local = NEXP // exp_count
    arrived_rows = lax.all_to_all(
        outgoing_rows.reshape(exp_count, expert_local * capacity, -1),
        "exp",
        split_axis=0,
        concat_axis=2,
        tiled=True,
    )
    gathered_in = arrived_rows.astype(jnp.float32)
    mean_square = jnp.mean(gathered_in * gathered_in, axis=-1, keepdims=True)
    normed = (gathered_in * lax.rsqrt(mean_square + EPS) * norm_gain).astype(jnp.bfloat16)
    rows_in = normed[0]
    model_width = rows_in.shape[1]
    cut = model_width // 2
    a_rows = ring_gather_whole(rows_in[:, :cut], lambda step: shift_pairs(side, 1, step))
    a_rows = ring_gather(jnp.stack(a_rows), side, 0)
    b_rows = ring_gather_whole(rows_in[:, cut:], lambda step: shift_pairs(side, 0, step))
    b_rows = ring_gather(jnp.stack(b_rows), side, 1)
    group_rows = side * capacity

    def half_dot(rows, weight):
        return jnp.dot(rows.reshape(group_rows, cut), weight, preferred_element_type=jnp.float32)

    def both_halves(weight):
        from_a = jnp.stack([half_dot(r, weight[:cut]) for r in a_rows])
        from_b = jnp.stack([half_dot(r, weight[cut:]) for r in b_rows])
        ff = weight.shape[1]
        return from_a.reshape(side, side, capacity, ff) + from_b.reshape(
            side, side, capacity, ff
        ).transpose(1, 0, 2, 3)

    gate_part = both_halves(w_gate[0])
    up_part = both_halves(w_up[0])
    hidden_units = (jax.nn.silu(gate_part) * up_part).astype(jnp.bfloat16)
    ff_local = hidden_units.shape[-1]

    def down_group(units, weight):
        return (
            jnp.dot(units.reshape(group_rows, ff_local), weight, preferred_element_type=jnp.float32)
            .astype(jnp.bfloat16)
            .reshape(side, capacity, cut)
        )

    far_group = side // 2
    far_a = down_group(hidden_units[far_group], w_down[0, :, :cut])
    far_b = down_group(hidden_units[:, far_group], w_down[0, :, cut:])
    far_a, far_b, units_rest = lax.optimization_barrier((far_a, far_b, hidden_units))
    down_a = [
        far_a if k == far_group else down_group(units_rest[k], w_down[0, :, :cut])
        for k in range(side)
    ]
    down_b = [
        far_b if k == far_group else down_group(units_rest[:, k], w_down[0, :, cut:])
        for k in range(side)
    ]
    part_a = ring_scatter(down_a, side, 0).astype(jnp.bfloat16)
    part_a = ring_scatter_whole([part_a[k] for k in range(side)], side, 1)
    part_b = ring_scatter(down_b, side, 1).astype(jnp.bfloat16)
    part_b = ring_scatter_whole([part_b[k] for k in range(side)], side, 0)
    returned = jnp.concatenate([part_a, part_b], axis=1).astype(jnp.bfloat16)
    outbound = returned.reshape(capacity, exp_count, model_width // exp_count).transpose(1, 0, 2)
    homed = lax.all_to_all(outbound, "exp", split_axis=0, concat_axis=0, tiled=True)
    lookup = homed.reshape(NEXP * capacity, -1)
    chosen = (
        lookup[slot_grid.reshape(assign_count)]
        .astype(jnp.float32)
        .reshape(tok_rows, top_count, -1)
    )
    gate_share = gate_probs / jnp.sum(gate_probs, axis=1, keepdims=True)
    layer_out = (
        residual.astype(jnp.float32) + jnp.sum(gate_share[:, :, None] * chosen, axis=1)
    ).astype(jnp.bfloat16)
    return (layer_out, cache_pages)


def solution(mesh):
    return jax.shard_map(
        per_device,
        mesh=mesh,
        in_specs=(
            P("seq", "exp"),
            P("seq", "exp"),
            P("seq", "exp"),
            P("seq", "exp"),
            P(),
            P(),
            P("exp", None),
            P(),
            P("seq", None),
            P("seq", None),
            P("exp", None, "seq"),
            P("exp", None, "seq"),
            P("exp", "seq", None),
        ),
        out_specs=(P("seq", "exp"), P("seq", None, None, "exp")),
        check_vma=False,
    )
```

```python
import math

import jax
import jax.numpy as jnp
from jax import lax
from jax.sharding import PartitionSpec as P

HEAD_SIZE = 128
NEXP = 8
PAGE_TOKENS = 16


THETA = 1000000.0
EPS = 1e-05


def apply_rotary(values_in, positions, head_count):
    row_count = values_in.shape[0]
    split_view = values_in.astype(jnp.float32).reshape(row_count, head_count, HEAD_SIZE)
    steps_half = jnp.arange(HEAD_SIZE // 2, dtype=jnp.float32)
    frequency = THETA ** (-(2.0 * steps_half) / HEAD_SIZE)
    angles = positions.astype(jnp.float32)[:, None] * frequency[None, :]
    cosine = jnp.cos(angles)[:, None, :]
    sine_part = jnp.sin(angles)[:, None, :]
    front_half = split_view[..., : HEAD_SIZE // 2]
    back_half = split_view[..., HEAD_SIZE // 2 :]
    turned = jnp.concatenate(
        [front_half * cosine - back_half * sine_part, back_half * cosine + front_half * sine_part],
        axis=-1,
    )
    return turned.reshape(row_count, head_count * HEAD_SIZE).astype(jnp.bfloat16)


def shift_pairs(side, along, step):
    pairs = []
    for src in range(side * side):
        a, b = divmod(src, side)
        if along == 0:
            dst = ((a + step) % side) * side + b
        else:
            dst = a * side + (b + step) % side
        pairs.append((src, dst))
    return pairs


def ring_gather_whole(piece, perm_of):
    from_minus = lax.ppermute(piece, "seq", perm_of(1))
    from_plus = lax.ppermute(piece, "seq", perm_of(-1))
    far = lax.ppermute(from_minus, "seq", perm_of(1))
    return [piece, from_plus, far, from_minus]


def exp_ring_pairs(zside, step):
    pairs = []
    for src in range(zside * 2):
        z, core = divmod(src, 2)
        pairs.append((src, ((z + step) % zside) * 2 + core))
    return pairs


def scatter_exp(partial, exp_count):
    rows, width = partial.shape
    zside = exp_count // 2
    block = width // exp_count
    exp_index = lax.axis_index("exp")
    my_z, my_core = exp_index // 2, exp_index % 2
    grid = partial.astype(jnp.bfloat16).reshape(rows, zside, 2, block)
    mine = lax.dynamic_index_in_dim(grid, my_core, axis=2, keepdims=False)
    theirs = lax.dynamic_index_in_dim(grid, 1 - my_core, axis=2, keepdims=False)
    swapped = lax.ppermute(theirs, "exp", [(e, e ^ 1) for e in range(exp_count)])
    chip_sum = (mine.astype(jnp.float32) + swapped.astype(jnp.float32)).astype(jnp.bfloat16)
    parts = [
        lax.dynamic_index_in_dim(chip_sum, (my_z + k) % zside, axis=1, keepdims=False)
        for k in range(zside)
    ]
    cut = rows // 2
    far = parts[2]
    got_m = lax.ppermute(far[:cut], "exp", exp_ring_pairs(zside, 1))
    got_p = lax.ppermute(far[cut:], "exp", exp_ring_pairs(zside, -1))
    near_p = parts[1].astype(jnp.float32)
    near_p = jnp.concatenate([near_p[:cut] + got_m.astype(jnp.float32), near_p[cut:]], axis=0)
    near_m = parts[3].astype(jnp.float32)
    near_m = jnp.concatenate([near_m[:cut], near_m[cut:] + got_p.astype(jnp.float32)], axis=0)
    recv_m = lax.ppermute(near_p.astype(jnp.bfloat16), "exp", exp_ring_pairs(zside, 1))
    recv_p = lax.ppermute(near_m.astype(jnp.bfloat16), "exp", exp_ring_pairs(zside, -1))
    return parts[0].astype(jnp.float32) + recv_m.astype(jnp.float32) + recv_p.astype(jnp.float32)


def ring_gather(piece, side, along):
    from_minus = lax.ppermute(piece, "seq", shift_pairs(side, along, 1))
    from_plus = lax.ppermute(piece, "seq", shift_pairs(side, along, -1))
    cut = piece.shape[-2] // 2
    far_a = lax.ppermute(from_minus[..., :cut, :], "seq", shift_pairs(side, along, 1))
    far_b = lax.ppermute(from_plus[..., cut:, :], "seq", shift_pairs(side, along, -1))
    far = jnp.concatenate([far_a, far_b], axis=-2)
    return [piece, from_plus, far, from_minus]


def gather_2d(piece_a, piece_b, side):
    a_rows = ring_gather(piece_a, side, 1)
    a_rows = ring_gather(jnp.stack(a_rows), side, 0)
    b_rows = ring_gather(piece_b, side, 0)
    b_rows = ring_gather(jnp.stack(b_rows), side, 1)
    return jnp.stack(a_rows), jnp.stack(b_rows, axis=1)


def ring_scatter(parts, side, along):
    cut = parts[0].shape[-2] // 2
    far = parts[2]
    got_m = lax.ppermute(far[..., :cut, :], "seq", shift_pairs(side, along, 1))
    got_p = lax.ppermute(far[..., cut:, :], "seq", shift_pairs(side, along, -1))
    near_p = parts[1].astype(jnp.float32)
    near_p = jnp.concatenate(
        [near_p[..., :cut, :] + got_m.astype(jnp.float32), near_p[..., cut:, :]], axis=-2
    )
    near_m = parts[3].astype(jnp.float32)
    near_m = jnp.concatenate(
        [near_m[..., :cut, :], near_m[..., cut:, :] + got_p.astype(jnp.float32)], axis=-2
    )
    recv_m = lax.ppermute(near_p.astype(jnp.bfloat16), "seq", shift_pairs(side, along, 1))
    recv_p = lax.ppermute(near_m.astype(jnp.bfloat16), "seq", shift_pairs(side, along, -1))
    return parts[0].astype(jnp.float32) + recv_m.astype(jnp.float32) + recv_p.astype(jnp.float32)


def scatter_2d(out_a, out_b, side):
    part_a = ring_scatter([out_a[k] for k in range(side)], side, 0).astype(jnp.bfloat16)
    part_a = ring_scatter([part_a[k] for k in range(side)], side, 1)
    part_b = ring_scatter([out_b[:, k] for k in range(side)], side, 1).astype(jnp.bfloat16)
    part_b = ring_scatter([part_b[k] for k in range(side)], side, 0)
    return part_a, part_b


def per_device(
    hidden,
    queries,
    keys,
    values,
    block_place,
    page_table,
    out_weight,
    norm_gain,
    gate_probs,
    routes,
    w_gate,
    w_up,
    w_down,
):
    seq_count = lax.axis_size("seq")
    exp_count = lax.axis_size("exp")
    seq_index = lax.axis_index("seq")
    tok_rows = queries.shape[0]
    half_rows = tok_rows // 2
    all_rows = tok_rows * seq_count
    long_len = 3 * all_rows // 4
    side = math.isqrt(seq_count)
    my_x, my_y = seq_index // side, seq_index % side
    block_count = block_place.shape[0]
    all_pos = (
        block_place[:, None] * half_rows + jnp.arange(half_rows, dtype=jnp.int32)[None, :]
    ).reshape(all_rows)
    my_pos = lax.dynamic_slice_in_dim(all_pos, seq_index * tok_rows, tok_rows)
    my_long = my_pos >= long_len
    my_rope = my_pos - long_len * my_long.astype(jnp.int32)
    q_heads = queries.shape[1] // HEAD_SIZE
    kv_heads = keys.shape[1] // HEAD_SIZE
    query_head_group = q_heads // kv_heads
    query_rotated = apply_rotary(queries, my_rope, q_heads)
    q_grid = query_rotated.reshape(tok_rows, kv_heads, query_head_group, HEAD_SIZE)
    score_scale = 1.0 / math.sqrt(HEAD_SIZE)
    page_count = tok_rows // PAGE_TOKENS
    page_total = page_table.shape[0]
    my_pages = seq_index * page_count + jnp.arange(page_count, dtype=jnp.int32)
    my_logical = jnp.sum(
        jnp.where(
            page_table[None, :] == my_pages[:, None],
            jnp.arange(page_total, dtype=jnp.int32)[None, :],
            0,
        ),
        axis=1,
    )
    slot_of_block = jnp.sum(
        jnp.where(
            block_place[None, :] == jnp.arange(block_count, dtype=jnp.int32)[:, None],
            jnp.arange(block_count, dtype=jnp.int32)[None, :],
            0,
        ),
        axis=1,
    )
    wanted_pos = (
        my_logical[:, None] * PAGE_TOKENS + jnp.arange(PAGE_TOKENS, dtype=jnp.int32)[None, :]
    ).reshape(page_count * PAGE_TOKENS)
    taken_abs = slot_of_block[wanted_pos // half_rows] * half_rows + wanted_pos % half_rows
    taken = taken_abs
    kv_width = keys.shape[1]
    kv_piece = jnp.concatenate([keys, values], axis=1)
    kv_all = lax.all_to_all(
        jnp.broadcast_to(kv_piece[None], (seq_count,) + kv_piece.shape),
        "seq",
        split_axis=0,
        concat_axis=0,
        tiled=True,
    ).reshape(all_rows, 2 * kv_width)
    all_rope = all_pos - long_len * (all_pos >= long_len).astype(jnp.int32)
    key_all = apply_rotary(kv_all[:, :kv_width], all_rope, kv_heads)
    value_all = kv_all[:, kv_width:]
    peak_old = jnp.full((kv_heads, query_head_group, tok_rows), -1e30, jnp.float32)
    row_count = key_all.shape[0]
    scores = (
        jnp.einsum(
            "tkgd,nkd->kgtn",
            q_grid,
            key_all.reshape(row_count, kv_heads, HEAD_SIZE),
            preferred_element_type=jnp.float32,
        )
        * score_scale
    )
    allowed = ((all_pos >= long_len)[None, :] == my_long[:, None]) & (
        all_pos[None, :] <= my_pos[:, None]
    )
    scores = jnp.where(allowed, scores, -1e30)
    peak_new = jnp.maximum(peak_old, jnp.max(scores, axis=-1))
    weights = jnp.where(allowed, jnp.exp(scores - peak_new[..., None]), 0.0)
    total_new = jnp.sum(weights, axis=-1)
    summed = jnp.einsum(
        "kgtn,nkd->kgtd",
        weights.astype(jnp.bfloat16),
        value_all.reshape(row_count, kv_heads, HEAD_SIZE),
        preferred_element_type=jnp.float32,
    )
    peak_final, total_final, summed = (peak_new, total_new, summed)
    cache_pages = jnp.stack([key_all[taken], value_all[taken]], axis=1).reshape(
        page_count, PAGE_TOKENS, 2, kv_heads * HEAD_SIZE
    )
    attended = (
        (summed / total_final[..., None])
        .transpose(2, 0, 1, 3)
        .reshape(tok_rows, q_heads * HEAD_SIZE)
        .astype(jnp.bfloat16)
    )
    partial_proj = jnp.dot(attended, out_weight, preferred_element_type=jnp.float32)
    projected = scatter_exp(partial_proj, exp_count)
    residual = (hidden.astype(jnp.float32) + projected).astype(jnp.bfloat16)
    top_count = routes.shape[1]
    capacity = tok_rows // 2
    assign_count = tok_rows * top_count
    flat_routes = routes.reshape(assign_count)
    expert_hot = (flat_routes[:, None] == jnp.arange(NEXP, dtype=jnp.int32)[None, :]).astype(
        jnp.float32
    )
    earlier = (jnp.arange(assign_count)[:, None] > jnp.arange(assign_count)[None, :]).astype(
        jnp.float32
    )
    before = jnp.dot(earlier, expert_hot, preferred_element_type=jnp.float32)
    slot_rank = jnp.sum(before * expert_hot, axis=1).astype(jnp.int32).reshape(tok_rows, top_count)
    slot_grid = routes * capacity + slot_rank
    chooser = jnp.any(
        slot_grid[None, :, :] == jnp.arange(NEXP * capacity, dtype=jnp.int32)[:, None, None],
        axis=-1,
    ).astype(jnp.bfloat16)
    outgoing_rows = jnp.dot(chooser, residual, preferred_element_type=jnp.float32).astype(
        jnp.bfloat16
    )
    expert_local = NEXP // exp_count
    arrived_rows = lax.all_to_all(
        outgoing_rows.reshape(exp_count, expert_local * capacity, -1),
        "exp",
        split_axis=0,
        concat_axis=2,
        tiled=True,
    )
    gathered_in = arrived_rows.astype(jnp.float32)
    mean_square = jnp.mean(gathered_in * gathered_in, axis=-1, keepdims=True)
    normed = (gathered_in * lax.rsqrt(mean_square + EPS) * norm_gain).astype(jnp.bfloat16)
    rows_in = normed[0]
    model_width = rows_in.shape[1]
    cut = model_width // 2
    a_rows = ring_gather(rows_in[:, :cut], side, 1)
    a_rows = ring_gather(jnp.stack(a_rows), side, 0)
    b_rows = ring_gather(rows_in[:, cut:], side, 0)
    b_rows = ring_gather(jnp.stack(b_rows), side, 1)
    group_rows = side * capacity

    def half_dot(rows, weight):
        return jnp.dot(rows.reshape(group_rows, cut), weight, preferred_element_type=jnp.float32)

    def both_halves(weight):
        from_a = jnp.stack([half_dot(r, weight[:cut]) for r in a_rows])
        from_b = jnp.stack([half_dot(r, weight[cut:]) for r in b_rows])
        ff = weight.shape[1]
        return from_a.reshape(side, side, capacity, ff) + from_b.reshape(
            side, side, capacity, ff
        ).transpose(1, 0, 2, 3)

    gate_part = both_halves(w_gate[0])
    up_part = both_halves(w_up[0])
    hidden_units = (jax.nn.silu(gate_part) * up_part).astype(jnp.bfloat16)
    ff_local = hidden_units.shape[-1]

    def down_group(units, weight):
        return (
            jnp.dot(units.reshape(group_rows, ff_local), weight, preferred_element_type=jnp.float32)
            .astype(jnp.bfloat16)
            .reshape(side, capacity, cut)
        )

    far_group = side // 2
    far_a = down_group(hidden_units[far_group], w_down[0, :, :cut])
    far_b = down_group(hidden_units[:, far_group], w_down[0, :, cut:])
    far_a, far_b, units_rest = lax.optimization_barrier((far_a, far_b, hidden_units))
    down_a = [
        far_a if k == far_group else down_group(units_rest[k], w_down[0, :, :cut])
        for k in range(side)
    ]
    down_b = [
        far_b if k == far_group else down_group(units_rest[:, k], w_down[0, :, cut:])
        for k in range(side)
    ]
    part_a = ring_scatter(down_a, side, 0).astype(jnp.bfloat16)
    part_a = ring_scatter([part_a[k] for k in range(side)], side, 1)
    part_b = ring_scatter(down_b, side, 1).astype(jnp.bfloat16)
    part_b = ring_scatter([part_b[k] for k in range(side)], side, 0)
    returned = jnp.concatenate([part_a, part_b], axis=1).astype(jnp.bfloat16)
    outbound = returned.reshape(capacity, exp_count, model_width // exp_count).transpose(1, 0, 2)
    homed = lax.all_to_all(outbound, "exp", split_axis=0, concat_axis=0, tiled=True)
    lookup = homed.reshape(NEXP * capacity, -1)
    chosen = (
        lookup[slot_grid.reshape(assign_count)]
        .astype(jnp.float32)
        .reshape(tok_rows, top_count, -1)
    )
    gate_share = gate_probs / jnp.sum(gate_probs, axis=1, keepdims=True)
    layer_out = (
        residual.astype(jnp.float32) + jnp.sum(gate_share[:, :, None] * chosen, axis=1)
    ).astype(jnp.bfloat16)
    return (layer_out, cache_pages)


def solution(mesh):
    return jax.shard_map(
        per_device,
        mesh=mesh,
        in_specs=(
            P("seq", "exp"),
            P("seq", "exp"),
            P("seq", "exp"),
            P("seq", "exp"),
            P(),
            P(),
            P("exp", None),
            P(),
            P("seq", None),
            P("seq", None),
            P("exp", None, "seq"),
            P("exp", None, "seq"),
            P("exp", "seq", None),
        ),
        out_specs=(P("seq", "exp"), P("seq", None, None, "exp")),
        check_vma=False,
    )
```

```python
import math

import jax
import jax.numpy as jnp
from jax import lax
from jax.sharding import PartitionSpec as P

HEAD_SIZE = 128
NEXP = 8
PAGE_TOKENS = 16


THETA = 1000000.0
EPS = 1e-05


def apply_rotary(values_in, positions, head_count):
    row_count = values_in.shape[0]
    split_view = values_in.astype(jnp.float32).reshape(row_count, head_count, HEAD_SIZE)
    steps_half = jnp.arange(HEAD_SIZE // 2, dtype=jnp.float32)
    frequency = THETA ** (-(2.0 * steps_half) / HEAD_SIZE)
    angles = positions.astype(jnp.float32)[:, None] * frequency[None, :]
    cosine = jnp.cos(angles)[:, None, :]
    sine_part = jnp.sin(angles)[:, None, :]
    front_half = split_view[..., : HEAD_SIZE // 2]
    back_half = split_view[..., HEAD_SIZE // 2 :]
    turned = jnp.concatenate(
        [front_half * cosine - back_half * sine_part, back_half * cosine + front_half * sine_part],
        axis=-1,
    )
    return turned.reshape(row_count, head_count * HEAD_SIZE).astype(jnp.bfloat16)


def shift_pairs(side, along, step):
    pairs = []
    for src in range(side * side):
        a, b = divmod(src, side)
        if along == 0:
            dst = ((a + step) % side) * side + b
        else:
            dst = a * side + (b + step) % side
        pairs.append((src, dst))
    return pairs


def ring_gather_whole(piece, perm_of):
    from_minus = lax.ppermute(piece, "seq", perm_of(1))
    from_plus = lax.ppermute(piece, "seq", perm_of(-1))
    far = lax.ppermute(from_minus, "seq", perm_of(1))
    return [piece, from_plus, far, from_minus]


def exp_ring_pairs(zside, step):
    pairs = []
    for src in range(zside * 2):
        z, core = divmod(src, 2)
        pairs.append((src, ((z + step) % zside) * 2 + core))
    return pairs


def scatter_exp(partial, exp_count):
    rows, width = partial.shape
    zside = exp_count // 2
    block = width // exp_count
    exp_index = lax.axis_index("exp")
    my_z, my_core = exp_index // 2, exp_index % 2
    grid = partial.astype(jnp.bfloat16).reshape(rows, zside, 2, block)
    mine = lax.dynamic_index_in_dim(grid, my_core, axis=2, keepdims=False)
    theirs = lax.dynamic_index_in_dim(grid, 1 - my_core, axis=2, keepdims=False)
    swapped = lax.ppermute(theirs, "exp", [(e, e ^ 1) for e in range(exp_count)])
    chip_sum = (mine.astype(jnp.float32) + swapped.astype(jnp.float32)).astype(jnp.bfloat16)
    parts = [
        lax.dynamic_index_in_dim(chip_sum, (my_z + k) % zside, axis=1, keepdims=False)
        for k in range(zside)
    ]
    cut = rows // 2
    far = parts[2]
    got_m = lax.ppermute(far[:cut], "exp", exp_ring_pairs(zside, 1))
    got_p = lax.ppermute(far[cut:], "exp", exp_ring_pairs(zside, -1))
    near_p = parts[1].astype(jnp.float32)
    near_p = jnp.concatenate([near_p[:cut] + got_m.astype(jnp.float32), near_p[cut:]], axis=0)
    near_m = parts[3].astype(jnp.float32)
    near_m = jnp.concatenate([near_m[:cut], near_m[cut:] + got_p.astype(jnp.float32)], axis=0)
    recv_m = lax.ppermute(near_p.astype(jnp.bfloat16), "exp", exp_ring_pairs(zside, 1))
    recv_p = lax.ppermute(near_m.astype(jnp.bfloat16), "exp", exp_ring_pairs(zside, -1))
    return parts[0].astype(jnp.float32) + recv_m.astype(jnp.float32) + recv_p.astype(jnp.float32)


def ring_gather(piece, side, along):
    from_minus = lax.ppermute(piece, "seq", shift_pairs(side, along, 1))
    from_plus = lax.ppermute(piece, "seq", shift_pairs(side, along, -1))
    cut = piece.shape[-2] // 2
    far_a = lax.ppermute(from_minus[..., :cut, :], "seq", shift_pairs(side, along, 1))
    far_b = lax.ppermute(from_plus[..., cut:, :], "seq", shift_pairs(side, along, -1))
    far = jnp.concatenate([far_a, far_b], axis=-2)
    return [piece, from_plus, far, from_minus]


def gather_2d(piece_a, piece_b, side):
    a_rows = ring_gather(piece_a, side, 1)
    a_rows = ring_gather(jnp.stack(a_rows), side, 0)
    b_rows = ring_gather(piece_b, side, 0)
    b_rows = ring_gather(jnp.stack(b_rows), side, 1)
    return jnp.stack(a_rows), jnp.stack(b_rows, axis=1)


def ring_scatter(parts, side, along):
    cut = parts[0].shape[-2] // 2
    far = parts[2]
    got_m = lax.ppermute(far[..., :cut, :], "seq", shift_pairs(side, along, 1))
    got_p = lax.ppermute(far[..., cut:, :], "seq", shift_pairs(side, along, -1))
    near_p = parts[1].astype(jnp.float32)
    near_p = jnp.concatenate(
        [near_p[..., :cut, :] + got_m.astype(jnp.float32), near_p[..., cut:, :]], axis=-2
    )
    near_m = parts[3].astype(jnp.float32)
    near_m = jnp.concatenate(
        [near_m[..., :cut, :], near_m[..., cut:, :] + got_p.astype(jnp.float32)], axis=-2
    )
    recv_m = lax.ppermute(near_p.astype(jnp.bfloat16), "seq", shift_pairs(side, along, 1))
    recv_p = lax.ppermute(near_m.astype(jnp.bfloat16), "seq", shift_pairs(side, along, -1))
    return parts[0].astype(jnp.float32) + recv_m.astype(jnp.float32) + recv_p.astype(jnp.float32)


def scatter_2d(out_a, out_b, side):
    part_a = ring_scatter([out_a[k] for k in range(side)], side, 0).astype(jnp.bfloat16)
    part_a = ring_scatter([part_a[k] for k in range(side)], side, 1)
    part_b = ring_scatter([out_b[:, k] for k in range(side)], side, 1).astype(jnp.bfloat16)
    part_b = ring_scatter([part_b[k] for k in range(side)], side, 0)
    return part_a, part_b


def per_device(
    hidden,
    queries,
    keys,
    values,
    block_place,
    page_table,
    out_weight,
    norm_gain,
    gate_probs,
    routes,
    w_gate,
    w_up,
    w_down,
):
    seq_count = lax.axis_size("seq")
    exp_count = lax.axis_size("exp")
    seq_index = lax.axis_index("seq")
    tok_rows = queries.shape[0]
    half_rows = tok_rows // 2
    all_rows = tok_rows * seq_count
    long_len = 3 * all_rows // 4
    side = math.isqrt(seq_count)
    my_x, my_y = seq_index // side, seq_index % side
    block_count = block_place.shape[0]
    all_pos = (
        block_place[:, None] * half_rows + jnp.arange(half_rows, dtype=jnp.int32)[None, :]
    ).reshape(all_rows)
    my_pos = lax.dynamic_slice_in_dim(all_pos, seq_index * tok_rows, tok_rows)
    my_long = my_pos >= long_len
    my_rope = my_pos - long_len * my_long.astype(jnp.int32)
    q_heads = queries.shape[1] // HEAD_SIZE
    kv_heads = keys.shape[1] // HEAD_SIZE
    query_head_group = q_heads // kv_heads
    query_rotated = apply_rotary(queries, my_rope, q_heads)
    key_rotated = apply_rotary(keys, my_rope, kv_heads)
    q_grid = query_rotated.reshape(tok_rows, kv_heads, query_head_group, HEAD_SIZE)
    score_scale = 1.0 / math.sqrt(HEAD_SIZE)
    page_count = tok_rows // PAGE_TOKENS
    page_total = page_table.shape[0]
    my_pages = seq_index * page_count + jnp.arange(page_count, dtype=jnp.int32)
    my_logical = jnp.sum(
        jnp.where(
            page_table[None, :] == my_pages[:, None],
            jnp.arange(page_total, dtype=jnp.int32)[None, :],
            0,
        ),
        axis=1,
    )
    slot_of_block = jnp.sum(
        jnp.where(
            block_place[None, :] == jnp.arange(block_count, dtype=jnp.int32)[:, None],
            jnp.arange(block_count, dtype=jnp.int32)[None, :],
            0,
        ),
        axis=1,
    )
    wanted_pos = (
        my_logical[:, None] * PAGE_TOKENS + jnp.arange(PAGE_TOKENS, dtype=jnp.int32)[None, :]
    ).reshape(page_count * PAGE_TOKENS)
    taken_abs = slot_of_block[wanted_pos // half_rows] * half_rows + wanted_pos % half_rows
    taken = taken_abs
    kv_width = key_rotated.shape[1]
    kv_piece = jnp.concatenate([key_rotated, values], axis=1)
    kv_all = lax.all_to_all(
        jnp.broadcast_to(kv_piece[None], (seq_count,) + kv_piece.shape),
        "seq",
        split_axis=0,
        concat_axis=0,
        tiled=True,
    ).reshape(all_rows, 2 * kv_width)
    key_all, value_all = kv_all[:, :kv_width], kv_all[:, kv_width:]
    peak_old = jnp.full((kv_heads, query_head_group, tok_rows), -1e30, jnp.float32)
    row_count = key_all.shape[0]
    scores = (
        jnp.einsum(
            "tkgd,nkd->kgtn",
            q_grid,
            key_all.reshape(row_count, kv_heads, HEAD_SIZE),
            preferred_element_type=jnp.float32,
        )
        * score_scale
    )
    allowed = ((all_pos >= long_len)[None, :] == my_long[:, None]) & (
        all_pos[None, :] <= my_pos[:, None]
    )
    scores = jnp.where(allowed, scores, -1e30)
    peak_new = jnp.maximum(peak_old, jnp.max(scores, axis=-1))
    weights = jnp.where(allowed, jnp.exp(scores - peak_new[..., None]), 0.0)
    total_new = jnp.sum(weights, axis=-1)
    summed = jnp.einsum(
        "kgtn,nkd->kgtd",
        weights.astype(jnp.bfloat16),
        value_all.reshape(row_count, kv_heads, HEAD_SIZE),
        preferred_element_type=jnp.float32,
    )
    peak_final, total_final, summed = (peak_new, total_new, summed)
    cache_pages = jnp.stack([key_all[taken], value_all[taken]], axis=1).reshape(
        page_count, PAGE_TOKENS, 2, kv_heads * HEAD_SIZE
    )
    attended = (
        (summed / total_final[..., None])
        .transpose(2, 0, 1, 3)
        .reshape(tok_rows, q_heads * HEAD_SIZE)
        .astype(jnp.bfloat16)
    )
    partial_proj = jnp.dot(attended, out_weight, preferred_element_type=jnp.float32)
    projected = scatter_exp(partial_proj, exp_count)
    residual = (hidden.astype(jnp.float32) + projected).astype(jnp.bfloat16)
    top_count = routes.shape[1]
    capacity = tok_rows // 2
    assign_count = tok_rows * top_count
    flat_routes = routes.reshape(assign_count)
    expert_hot = (flat_routes[:, None] == jnp.arange(NEXP, dtype=jnp.int32)[None, :]).astype(
        jnp.float32
    )
    earlier = (jnp.arange(assign_count)[:, None] > jnp.arange(assign_count)[None, :]).astype(
        jnp.float32
    )
    before = jnp.dot(earlier, expert_hot, preferred_element_type=jnp.float32)
    slot_rank = jnp.sum(before * expert_hot, axis=1).astype(jnp.int32).reshape(tok_rows, top_count)
    slot_grid = routes * capacity + slot_rank
    chooser = jnp.any(
        slot_grid[None, :, :] == jnp.arange(NEXP * capacity, dtype=jnp.int32)[:, None, None],
        axis=-1,
    ).astype(jnp.bfloat16)
    outgoing_rows = jnp.dot(chooser, residual, preferred_element_type=jnp.float32).astype(
        jnp.bfloat16
    )
    expert_local = NEXP // exp_count
    arrived_rows = lax.all_to_all(
        outgoing_rows.reshape(exp_count, expert_local * capacity, -1),
        "exp",
        split_axis=0,
        concat_axis=2,
        tiled=True,
    )
    gathered_in = arrived_rows.astype(jnp.float32)
    mean_square = jnp.mean(gathered_in * gathered_in, axis=-1, keepdims=True)
    normed = (gathered_in * lax.rsqrt(mean_square + EPS) * norm_gain).astype(jnp.bfloat16)
    rows_in = normed[0]
    model_width = rows_in.shape[1]
    cut = model_width // 2
    a_rows = ring_gather(rows_in[:, :cut], side, 1)
    a_rows = ring_gather(jnp.stack(a_rows), side, 0)
    b_rows = ring_gather(rows_in[:, cut:], side, 0)
    b_rows = ring_gather(jnp.stack(b_rows), side, 1)
    group_rows = side * capacity

    def half_dot(rows, weight):
        return jnp.dot(rows.reshape(group_rows, cut), weight, preferred_element_type=jnp.float32)

    def both_halves(weight):
        from_a = jnp.stack([half_dot(r, weight[:cut]) for r in a_rows])
        from_b = jnp.stack([half_dot(r, weight[cut:]) for r in b_rows])
        ff = weight.shape[1]
        return from_a.reshape(side, side, capacity, ff) + from_b.reshape(
            side, side, capacity, ff
        ).transpose(1, 0, 2, 3)

    gate_part = both_halves(w_gate[0])
    up_part = both_halves(w_up[0])
    hidden_units = (jax.nn.silu(gate_part) * up_part).astype(jnp.bfloat16)
    ff_local = hidden_units.shape[-1]

    def down_group(units, weight):
        return (
            jnp.dot(units.reshape(group_rows, ff_local), weight, preferred_element_type=jnp.float32)
            .astype(jnp.bfloat16)
            .reshape(side, capacity, cut)
        )

    far_group = side // 2
    far_a = down_group(hidden_units[far_group], w_down[0, :, :cut])
    far_b = down_group(hidden_units[:, far_group], w_down[0, :, cut:])
    far_a, far_b, units_rest = lax.optimization_barrier((far_a, far_b, hidden_units))
    near_groups = [k for k in range(side) if k != far_group]

    def down_near(units, weight):
        return (
            jnp.dot(units.reshape(-1, ff_local), weight, preferred_element_type=jnp.float32)
            .astype(jnp.bfloat16)
            .reshape(len(near_groups), side, capacity, cut)
        )

    near_a = down_near(jnp.stack([units_rest[k] for k in near_groups]), w_down[0, :, :cut])
    near_b = down_near(jnp.stack([units_rest[:, k] for k in near_groups]), w_down[0, :, cut:])
    down_a = [far_a if k == far_group else near_a[near_groups.index(k)] for k in range(side)]
    down_b = [far_b if k == far_group else near_b[near_groups.index(k)] for k in range(side)]
    part_a = ring_scatter(down_a, side, 0).astype(jnp.bfloat16)
    part_a = ring_scatter([part_a[k] for k in range(side)], side, 1)
    part_b = ring_scatter(down_b, side, 1).astype(jnp.bfloat16)
    part_b = ring_scatter([part_b[k] for k in range(side)], side, 0)
    returned = jnp.concatenate([part_a, part_b], axis=1).astype(jnp.bfloat16)
    outbound = returned.reshape(capacity, exp_count, model_width // exp_count).transpose(1, 0, 2)
    homed = lax.all_to_all(outbound, "exp", split_axis=0, concat_axis=0, tiled=True)
    lookup = homed.reshape(NEXP * capacity, -1)
    chosen = (
        lookup[slot_grid.reshape(assign_count)]
        .astype(jnp.float32)
        .reshape(tok_rows, top_count, -1)
    )
    gate_share = gate_probs / jnp.sum(gate_probs, axis=1, keepdims=True)
    layer_out = (
        residual.astype(jnp.float32) + jnp.sum(gate_share[:, :, None] * chosen, axis=1)
    ).astype(jnp.bfloat16)
    return (layer_out, cache_pages)


def solution(mesh):
    return jax.shard_map(
        per_device,
        mesh=mesh,
        in_specs=(
            P("seq", "exp"),
            P("seq", "exp"),
            P("seq", "exp"),
            P("seq", "exp"),
            P(),
            P(),
            P("exp", None),
            P(),
            P("seq", None),
            P("seq", None),
            P("exp", None, "seq"),
            P("exp", None, "seq"),
            P("exp", "seq", None),
        ),
        out_specs=(P("seq", "exp"), P("seq", None, None, "exp")),
        check_vma=False,
    )
```
